256 devices in a mesh: mom: 64 (over z, x, core), en: 4 (over y).
Axes of the slice: x: 4, y: 4, z: 8, core: 2. Of those that a mesh axis runs over, the one named last changes fastest.
Arguments:
- slab_inverse: float32 [64, 8, 2, 2, 128, 128], P('mom', 'en')
- coupling: float32 [64, 2, 2, 128, 128], P('mom'), may hold values from -0.125 to 0.125
- injection: float32 [64, 8, 2, 128], P('mom', 'en'), may hold values from 0.2 to 2
- neighbors: int32 [2, 128, 32], replicated, may hold values from 0 to 127
- mode_shift: int32 [6], replicated, may hold values from 1 to 2, as said below
- mode_table: int32 [64, 64], P('mom'), may hold values from 0 to 5
- emit_weight: float32 [6], replicated, may hold values from 0.3 to 3
- absorb_weight: float32 [6], replicated, may hold values from 0.3 to 3
Outputs:
- self_energy: float32 [64, 8, 64, 2, 128], P('mom', 'en')
The draws below stay inside these ranges and needn't reach their ends.
Inputs may be any that keep to these rules, and one draw needn't show every extreme that they name: `mode_shift`: some branch shifts by 2 grid steps and some by 1.
All inputs are finite; a program needn't handle non-finite values.
Results may differ from the reference program's by a relative error of at most 0.0003.
Values sent between devices are 32-bit elements; how exact they have to be, the bound alone decides.
No kernel may reach another device: no remote copies, remote signals or barrier semaphores. Data moves between devices by JAX's collectives and lax.ppermute only.
A program may use at most 128 MiB of HBM per device.

```python
import math
import jax
import jax.numpy as jnp
from jax import lax

ORB = 128
SLABS = 2
NBRS = 32
MODES = 6
SHIFT_MAX = 2
MOMENTA = 64
ENERGIES = 8


def draw_slab_inverse(key, part):
    first, second, third = jax.random.split(key, 3)
    shape = (MOMENTA, ENERGIES, SLABS, 2, ORB, ORB)
    rough = jax.random.normal(first, shape, jnp.float32) * (0.3 / ORB ** 0.5)
    diag_shape = (MOMENTA, ENERGIES, SLABS, 1, ORB)
    real_diag = jax.random.uniform(second, diag_shape, jnp.float32, -0.8, 0.8)
    imag_diag = -jax.random.uniform(third, diag_shape, jnp.float32, 0.3, 1.0)
    diagonal = jnp.concatenate([real_diag, imag_diag], axis=3)[..., None, :]
    return rough + diagonal * jnp.eye(ORB, dtype=jnp.float32)


def draw_mode_shift(key, part):
    first, second = jax.random.split(jax.random.fold_in(key, 7), 2)
    shifts = jax.random.randint(first, (MODES,), 1, SHIFT_MAX + 1)
    order = jax.random.permutation(second, MODES)
    shifts = shifts.at[order[0]].set(SHIFT_MAX)
    shifts = shifts.at[order[1]].set(1)
    return shifts.astype(jnp.int32)


def set_ends(entries, stream_key, least, largest):
    longest = entries.shape.index(max(entries.shape))
    spots = []
    for shift in (0, 1):
        where = [jax.random.randint(jax.random.fold_in(stream_key, axis), (), 0, length) for axis, length in enumerate(entries.shape)]
        where[longest] = (where[longest] + shift) % entries.shape[longest]
        spots.append(tuple(where))
    return entries.at[spots[0]].set(least).at[spots[1]].set(largest)


def block_scale(own_key, dims, cuts, least, largest):
    level, own = 1.0, jax.random.fold_in(own_key, 6)
    for position, blocks in cuts:
        heights = jnp.exp(jax.random.uniform(jax.random.fold_in(own, position), (blocks,), jnp.float32, least / len(cuts), largest / len(cuts)))
        level = level * jnp.repeat(heights, dims[position] // blocks).reshape([-1 if axis == position else 1 for axis in range(len(dims))])
    return level


def bell_draw(rng, shape, width, most, shards=(), kind=jnp.bfloat16):
    array = jax.random.normal(rng, shape, jnp.float32) * width
    if len(shards) > 0:
        array = block_scale(rng, shape, shards, -0.22, 0.18) * array
    return jnp.clip(array, min=-most, max=most).astype(kind)


def setup_inputs(seed: int = 0) -> dict:
    keys = jax.random.split(jax.random.key(seed), 9)
    slab_inverse = draw_slab_inverse(jax.random.fold_in(keys[8], 71), 0)
    coupling = bell_draw(keys[1], (MOMENTA, SLABS, 2, ORB, ORB), (16 * ORB) ** -0.5, 0.125, ((0, 64),), jnp.float32)
    injection = jnp.clip(jnp.exp(math.log(2.0) - 2.3025851 * jax.random.uniform(keys[2], (MOMENTA, ENERGIES, SLABS, ORB), jnp.float32) ** block_scale(keys[2], (MOMENTA, ENERGIES, SLABS, ORB), ((0, 64), (1, 4)), -0.2, 0.2)), 0.2, 2.0)
    neighbors = set_ends(jax.random.randint(keys[3], (SLABS, ORB, NBRS), 0, ORB), jax.random.fold_in(keys[3], 1), 0, ORB - 1).astype(jnp.int32)
    mode_shift = draw_mode_shift(jax.random.fold_in(keys[8], 71), 0)
    mode_table = set_ends(jax.random.randint(keys[5], (MOMENTA, MOMENTA), 0, MODES), jax.random.fold_in(keys[5], 1), 0, MODES - 1).astype(jnp.int32)
    emit_weight = jnp.clip(jnp.exp(jax.random.uniform(keys[6], (MODES,), jnp.float32, math.log(0.3), math.log(3.0))), 0.3, 3.0)
    absorb_weight = jnp.clip(jnp.exp(jax.random.uniform(keys[7], (MODES,), jnp.float32, math.log(0.3), math.log(3.0))), 0.3, 3.0)
    return dict(slab_inverse=slab_inverse, coupling=coupling, injection=injection, neighbors=neighbors, mode_shift=mode_shift, mode_table=mode_table, emit_weight=emit_weight, absorb_weight=absorb_weight)


HIGH = lax.Precision.HIGHEST


def product(left, right):
    return jnp.einsum("...ij,...jk->...ik", left, right, precision=HIGH)


def cmul(first, second):
    return (product(first[0], second[0]) - product(first[1], second[1]),
            product(first[0], second[1]) + product(first[1], second[0]))


def adjoint(value):
    return (jnp.swapaxes(value[0], -1, -2), -jnp.swapaxes(value[1], -1, -2))


def slab_pairs(slab_inverse, coupling, injection, neighbors):
    eye = jnp.eye(ORB, dtype=jnp.float32)
    collected = []
    retarded = None
    lesser = None
    for slab in range(SLABS):
        inverse = (slab_inverse[:, slab, 0], slab_inverse[:, slab, 1])
        source = injection[:, slab][:, None, :]
        if slab == 0:
            retarded = inverse
            lesser = cmul((retarded[0] * source, retarded[1] * source), adjoint(retarded))
        else:
            link = (coupling[slab, 0], coupling[slab, 1])
            back = adjoint(link)
            sigma = cmul(cmul(link, retarded), back)
            inner = cmul(cmul(inverse, sigma), inverse)
            retarded = (inverse[0] + inner[0], inverse[1] + inner[1])
            middle = cmul(cmul(link, lesser), back)
            middle = (middle[0] + eye[None] * source, middle[1])
            lesser = cmul(cmul(retarded, middle), adjoint(retarded))
        index = jnp.broadcast_to(neighbors[slab][None], (lesser[0].shape[0],) + neighbors[slab].shape)
        parts = [jnp.take_along_axis(value, index, axis=-1) for value in lesser]
        stacked = jnp.stack(parts, axis=1)
        collected.append(jnp.transpose(stacked, (0, 3, 1, 2)))
    return jnp.concatenate(collected, axis=1)


def reference(slab_inverse, coupling, injection, neighbors, mode_shift, mode_table, emit_weight, absorb_weight):
    def per_momentum(items):
        return slab_pairs(items[0], items[1], items[2], neighbors)

    pairs = lax.map(per_momentum, (slab_inverse, coupling, injection))
    padded = jnp.pad(pairs, ((0, 0), (SHIFT_MAX, SHIFT_MAX), (0, 0), (0, 0), (0, 0)))

    def convolve_one(table_row):
        def add_one(source, total):
            mode = table_row[source]
            shift = mode_shift[mode].astype(jnp.int32)
            block = padded[source]
            lower = lax.dynamic_slice_in_dim(block, (SHIFT_MAX - shift).astype(jnp.int32), ENERGIES, 0)
            upper = lax.dynamic_slice_in_dim(block, (SHIFT_MAX + shift).astype(jnp.int32), ENERGIES, 0)
            return total + emit_weight[mode] * lower + absorb_weight[mode] * upper

        start = jnp.zeros(pairs.shape[1:], jnp.float32)
        total = lax.fori_loop(0, MOMENTA, add_one, start)
        return total / MOMENTA

    return lax.map(convolve_one, mode_table)
```

```python
import jax
import jax.numpy as jnp
from jax import lax
from jax.sharding import PartitionSpec as P

SHIFT_MAX = 2
OFFSETS = (-2, -1, 1, 2)


HIGH = lax.Precision.HIGHEST


def with_halo(x, sides, width):
    for axis, dim in sides:
        count, length = (lax.axis_size(axis), x.shape[dim])
        up = [(i, (i + 1) % count) for i in range(count - 1)]
        down = [(j, i) for i, j in up]
        last = lax.slice_in_dim(x, length - width, length, axis=dim)
        leading = lax.slice_in_dim(x, 0, width, axis=dim)
        before = lax.ppermute(last, axis, up)
        after = lax.ppermute(leading, axis, down)
        x = jnp.concatenate([before, x, after], axis=dim)
    return x


def product(left, right):
    return jnp.einsum("...ij,...jk->...ik", left, right, precision=HIGH)


def cmul(first, second):
    return (
        product(first[0], second[0]) - product(first[1], second[1]),
        product(first[0], second[1]) + product(first[1], second[0]),
    )


def adjoint(value):
    return (jnp.swapaxes(value[0], -1, -2), -jnp.swapaxes(value[1], -1, -2))


def slab_pairs(slab_inverse, coupling, injection, neighbors):
    orbitals = slab_inverse.shape[-1]
    slab_count = slab_inverse.shape[1]
    eye = jnp.eye(orbitals, dtype=jnp.float32)
    columns = jnp.arange(orbitals, dtype=jnp.int32)
    collected = []
    retarded = None
    lesser = None
    for slab in range(slab_count):
        inverse = (slab_inverse[:, slab, 0], slab_inverse[:, slab, 1])
        source = injection[:, slab][:, None, :]
        if slab == 0:
            retarded = inverse
            lesser = cmul((retarded[0] * source, retarded[1] * source), adjoint(retarded))
        else:
            link = (coupling[slab, 0], coupling[slab, 1])
            back = adjoint(link)
            sigma = cmul(cmul(link, retarded), back)
            inner = cmul(cmul(inverse, sigma), inverse)
            retarded = (inverse[0] + inner[0], inverse[1] + inner[1])
            middle = cmul(cmul(link, lesser), back)
            middle = (middle[0] + eye[None] * source, middle[1])
            lesser = cmul(cmul(retarded, middle), adjoint(retarded))
        selector = (neighbors[slab][:, :, None] == columns[None, None, :]).astype(jnp.float32)
        parts = [jnp.einsum("eoc,ojc->ejo", value, selector, precision=HIGH) for value in lesser]
        collected.append(jnp.stack(parts, axis=2))
    return jnp.concatenate(collected, axis=1)


def shift_weights(table_row, mode_shift, emit_weight, absorb_weight):
    mode_ids = jnp.arange(mode_shift.shape[0], dtype=jnp.int32)
    chosen = (table_row[:, None] == mode_ids[None, :]).astype(jnp.float32)
    shift = jnp.sum(chosen * mode_shift.astype(jnp.float32)[None], axis=1)
    emit = jnp.sum(chosen * emit_weight[None], axis=1)
    absorb = jnp.sum(chosen * absorb_weight[None], axis=1)
    rows = []
    for offset in OFFSETS:
        if offset < 0:
            rows.append(emit * (shift == -offset).astype(jnp.float32))
        else:
            rows.append(absorb * (shift == offset).astype(jnp.float32))
    return jnp.stack(rows) / table_row.shape[0]


def mix(data, weights, energies):
    total = None
    for index, offset in enumerate(OFFSETS):
        window = data[SHIFT_MAX + offset : SHIFT_MAX + offset + energies]
        term = jnp.einsum("kj,ejc->kec", weights[:, index], window, precision=HIGH)
        total = term if total is None else total + term
    return total


def shards(
    slab_inverse, coupling, injection, neighbors, mode_shift, mode_table, emit_weight, absorb_weight
):
    pairs = slab_pairs(slab_inverse[0], coupling[0], injection[0], neighbors)
    energies = pairs.shape[0]
    moms = lax.axis_size("mom")
    flat = pairs.reshape(energies, -1)
    width = flat.shape[1] // moms
    widened = with_halo(flat, (("en", 0),), SHIFT_MAX)
    blocks = widened.reshape(widened.shape[0], moms, width)
    weights = shift_weights(mode_table[0], mode_shift, emit_weight, absorb_weight).reshape(-1)
    extra = -(-weights.shape[0] // width)
    weights = jnp.pad(weights, (0, extra * width - weights.shape[0]))
    rows = jnp.broadcast_to(weights.reshape(extra, 1, width), (extra, moms, width))
    sent = lax.all_to_all(jnp.concatenate([blocks, rows], axis=0), "mom", 1, 1)
    data = sent[: widened.shape[0]]
    table = jnp.swapaxes(sent[widened.shape[0] :], 0, 1).reshape(moms, -1)
    table = table[:, : len(OFFSETS) * moms].reshape(moms, len(OFFSETS), moms)
    mixed = mix(data, table, energies)
    back = lax.all_to_all(mixed, "mom", 0, 0)
    result = jnp.swapaxes(back, 0, 1).reshape(pairs.shape)
    return result[None]


def solution(mesh):
    placed = (
        P("mom", "en", None, None, None, None),
        P("mom", None, None, None, None),
        P("mom", "en", None, None),
        P(),
        P(),
        P("mom", None),
        P(),
        P(),
    )
    return jax.shard_map(
        shards,
        mesh=mesh,
        in_specs=placed,
        out_specs=P("mom", "en", None, None, None),
        check_vma=False,
    )
```

```python
import jax
import jax.numpy as jnp
from jax import lax
from jax.sharding import PartitionSpec as P

SHIFT_MAX = 2
OFFSETS = (-2, -1, 1, 2)


HIGH = lax.Precision.HIGHEST


def with_halo(x, sides, width):
    for axis, dim in sides:
        count, length = (lax.axis_size(axis), x.shape[dim])
        up = [(i, (i + 1) % count) for i in range(count - 1)]
        down = [(j, i) for i, j in up]
        last = lax.slice_in_dim(x, length - width, length, axis=dim)
        leading = lax.slice_in_dim(x, 0, width, axis=dim)
        before = lax.ppermute(last, axis, up)
        after = lax.ppermute(leading, axis, down)
        x = jnp.concatenate([before, x, after], axis=dim)
    return x


def product(left, right):
    return jnp.einsum("...ij,...jk->...ik", left, right, precision=HIGH)


def cmul(first, second):
    return (
        product(first[0], second[0]) - product(first[1], second[1]),
        product(first[0], second[1]) + product(first[1], second[0]),
    )


def adjoint(value):
    return (jnp.swapaxes(value[0], -1, -2), -jnp.swapaxes(value[1], -1, -2))


def slab_pairs(slab_inverse, coupling, injection, neighbors):
    orbitals = slab_inverse.shape[-1]
    slab_count = slab_inverse.shape[1]
    eye = jnp.eye(orbitals, dtype=jnp.float32)
    columns = jnp.arange(orbitals, dtype=jnp.int32)
    collected = []
    retarded = None
    lesser = None
    for slab in range(slab_count):
        inverse = (slab_inverse[:, slab, 0], slab_inverse[:, slab, 1])
        source = injection[:, slab][:, None, :]
        if slab == 0:
            retarded = inverse
            lesser = cmul((retarded[0] * source, retarded[1] * source), adjoint(retarded))
        else:
            link = (coupling[slab, 0], coupling[slab, 1])
            back = adjoint(link)
            sigma = cmul(cmul(link, retarded), back)
            inner = cmul(cmul(inverse, sigma), inverse)
            retarded = (inverse[0] + inner[0], inverse[1] + inner[1])
            middle = cmul(cmul(link, lesser), back)
            middle = (middle[0] + eye[None] * source, middle[1])
            lesser = cmul(cmul(retarded, middle), adjoint(retarded))
        selector = (neighbors[slab][:, :, None] == columns[None, None, :]).astype(jnp.float32)
        parts = [jnp.einsum("eoc,ojc->ejo", value, selector, precision=HIGH) for value in lesser]
        collected.append(jnp.stack(parts, axis=2))
    return jnp.concatenate(collected, axis=1)


def shift_weights(table_row, mode_shift, emit_weight, absorb_weight):
    mode_ids = jnp.arange(mode_shift.shape[0], dtype=jnp.int32)
    chosen = (table_row[:, None] == mode_ids[None, :]).astype(jnp.float32)
    shift = jnp.sum(chosen * mode_shift.astype(jnp.float32)[None], axis=1)
    emit = jnp.sum(chosen * emit_weight[None], axis=1)
    absorb = jnp.sum(chosen * absorb_weight[None], axis=1)
    rows = []
    for offset in OFFSETS:
        if offset < 0:
            rows.append(emit * (shift == -offset).astype(jnp.float32))
        else:
            rows.append(absorb * (shift == offset).astype(jnp.float32))
    return jnp.stack(rows) / table_row.shape[0]


def mix(data, weights, energies):
    total = None
    for index, offset in enumerate(OFFSETS):
        window = data[:, SHIFT_MAX + offset : SHIFT_MAX + offset + energies]
        term = jnp.einsum("kj,jec->kec", weights[:, index], window, precision=HIGH)
        total = term if total is None else total + term
    return total


def shards(
    slab_inverse, coupling, injection, neighbors, mode_shift, mode_table, emit_weight, absorb_weight
):
    pairs = slab_pairs(slab_inverse[0], coupling[0], injection[0], neighbors)
    local = pairs.shape[0]
    moms, groups = lax.axis_size("mom"), lax.axis_size("en")
    devices = moms * groups
    flat = pairs.reshape(local, -1)
    width = flat.shape[1] // devices
    blocks = jnp.swapaxes(flat.reshape(local, devices, width), 0, 1)
    weights = shift_weights(mode_table[0], mode_shift, emit_weight, absorb_weight).reshape(-1)
    share = -(-weights.shape[0] // (groups * width)) * width
    weights = jnp.pad(weights, (0, share * groups - weights.shape[0]))
    mine = lax.dynamic_slice_in_dim(weights, lax.axis_index("en") * share, share)
    rows = jnp.broadcast_to(mine.reshape(1, -1, width), (devices, share // width, width))
    sent = lax.all_to_all(jnp.concatenate([blocks, rows], axis=1), ("mom", "en"), 0, 0)
    sent = sent.reshape(moms, groups, local + share // width, width)
    data = sent[:, :, :local].reshape(moms, groups * local, width)
    data = jnp.pad(data, ((0, 0), (SHIFT_MAX, SHIFT_MAX), (0, 0)))
    table = sent[:, :, local:].reshape(moms, -1)[:, : len(OFFSETS) * moms]
    mixed = mix(data, table.reshape(moms, len(OFFSETS), moms), groups * local)
    mixed = mixed.reshape(devices, local, width)
    back = lax.all_to_all(mixed, ("mom", "en"), 0, 0)
    result = jnp.swapaxes(back, 0, 1).reshape(pairs.shape)
    return result[None]


def solution(mesh):
    placed = (
        P("mom", "en", None, None, None, None),
        P("mom", None, None, None, None),
        P("mom", "en", None, None),
        P(),
        P(),
        P("mom", None),
        P(),
        P(),
    )
    return jax.shard_map(
        shards,
        mesh=mesh,
        in_specs=placed,
        out_specs=P("mom", "en", None, None, None),
        check_vma=False,
    )
```

```python
import jax
import jax.numpy as jnp
from jax import lax
from jax.sharding import PartitionSpec as P

SHIFT_MAX = 2
OFFSETS = (-2, -1, 1, 2)


HIGH = lax.Precision.HIGHEST


def with_halo(x, sides, width):
    for axis, dim in sides:
        count, length = (lax.axis_size(axis), x.shape[dim])
        up = [(i, (i + 1) % count) for i in range(count - 1)]
        down = [(j, i) for i, j in up]
        last = lax.slice_in_dim(x, length - width, length, axis=dim)
        leading = lax.slice_in_dim(x, 0, width, axis=dim)
        before = lax.ppermute(last, axis, up)
        after = lax.ppermute(leading, axis, down)
        x = jnp.concatenate([before, x, after], axis=dim)
    return x


def block(value):
    real, imag = value[..., 0, :, :], value[..., 1, :, :]
    top = jnp.concatenate([real, -imag], axis=-1)
    bottom = jnp.concatenate([imag, real], axis=-1)
    return jnp.concatenate([top, bottom], axis=-2)


def column(value, adjoint=False):
    real, imag = value[..., 0, :, :], value[..., 1, :, :]
    if adjoint:
        real, imag = jnp.swapaxes(real, -1, -2), -jnp.swapaxes(imag, -1, -2)
    return jnp.concatenate([real, imag], axis=-2)


def split(value):
    rows = value.shape[-2] // 2
    return value.reshape(value.shape[:-2] + (2, rows, value.shape[-1]))


def cmul(left, right, spec="...ij,...jk->...ik", adjoint=False):
    product = jnp.einsum(spec, block(left), column(right, adjoint), precision=HIGH)
    return split(product)


def slab_pairs(slab_inverse, coupling, injection, neighbors):
    orbitals = slab_inverse.shape[-1]
    slab_count = slab_inverse.shape[1]
    eye = jnp.eye(orbitals, dtype=jnp.float32)
    retarded = slab_inverse[:, 0]
    source = injection[:, 0][:, None, None, :]
    lesser = cmul(retarded * source, retarded, adjoint=True)
    collected = [lesser]
    for slab in range(1, slab_count):
        inverse = slab_inverse[:, slab]
        link = coupling[slab]
        both = jnp.concatenate([retarded, lesser], axis=-1)
        linked = cmul(link, both, "ij,ejk->eik")
        linked = jnp.stack([linked[..., :orbitals], linked[..., orbitals:]], axis=1)
        sandwich = cmul(linked, link, "ewij,jk->ewik", adjoint=True)
        sigma, middle = sandwich[:, 0], sandwich[:, 1]
        diagonal = eye[None] * injection[:, slab][:, None, :]
        middle = jnp.stack([middle[:, 0] + diagonal, middle[:, 1]], axis=1)
        inner = cmul(cmul(inverse, sigma), inverse)
        retarded = inverse + inner
        lesser = cmul(cmul(retarded, middle), retarded, adjoint=True)
        collected.append(lesser)
    stacked = jnp.stack(collected, axis=1)
    index = jnp.broadcast_to(
        neighbors[None, :, None, :, :], stacked.shape[:3] + neighbors.shape[1:]
    )
    picked = jnp.take_along_axis(stacked, index, axis=-1)
    picked = jnp.transpose(picked, (0, 1, 4, 2, 3))
    return picked.reshape(picked.shape[0], -1, picked.shape[3], picked.shape[4])


def shift_weights(table_row, mode_shift, emit_weight, absorb_weight):
    mode_ids = jnp.arange(mode_shift.shape[0], dtype=jnp.int32)
    chosen = (table_row[:, None] == mode_ids[None, :]).astype(jnp.float32)
    shift = jnp.sum(chosen * mode_shift.astype(jnp.float32)[None], axis=1)
    emit = jnp.sum(chosen * emit_weight[None], axis=1)
    absorb = jnp.sum(chosen * absorb_weight[None], axis=1)
    rows = []
    for offset in OFFSETS:
        if offset < 0:
            rows.append(emit * (shift == -offset).astype(jnp.float32))
        else:
            rows.append(absorb * (shift == offset).astype(jnp.float32))
    return jnp.stack(rows) / table_row.shape[0]


def mix(data, weights, energies):
    total = None
    for index, offset in enumerate(OFFSETS):
        window = data[:, SHIFT_MAX + offset : SHIFT_MAX + offset + energies]
        term = jnp.einsum("kj,jec->kec", weights[:, index], window, precision=HIGH)
        total = term if total is None else total + term
    return total


def shards(
    slab_inverse, coupling, injection, neighbors, mode_shift, mode_table, emit_weight, absorb_weight
):
    pairs = slab_pairs(slab_inverse[0], coupling[0], injection[0], neighbors)
    local = pairs.shape[0]
    moms, groups = lax.axis_size("mom"), lax.axis_size("en")
    devices = moms * groups
    flat = pairs.reshape(local, -1)
    width = flat.shape[1] // devices
    blocks = jnp.swapaxes(flat.reshape(local, devices, width), 0, 1)
    weights = shift_weights(mode_table[0], mode_shift, emit_weight, absorb_weight).reshape(-1)
    share = -(-weights.shape[0] // (groups * width)) * width
    weights = jnp.pad(weights, (0, share * groups - weights.shape[0]))
    mine = lax.dynamic_slice_in_dim(weights, lax.axis_index("en") * share, share)
    rows = jnp.broadcast_to(mine.reshape(1, -1, width), (devices, share // width, width))
    sent = lax.all_to_all(jnp.concatenate([blocks, rows], axis=1), ("mom", "en"), 0, 0)
    sent = sent.reshape(moms, groups, local + share // width, width)
    data = sent[:, :, :local].reshape(moms, groups * local, width)
    data = jnp.pad(data, ((0, 0), (SHIFT_MAX, SHIFT_MAX), (0, 0)))
    table = sent[:, :, local:].reshape(moms, -1)[:, : len(OFFSETS) * moms]
    mixed = mix(data, table.reshape(moms, len(OFFSETS), moms), groups * local)
    mixed = mixed.reshape(devices, local, width)
    back = lax.all_to_all(mixed, ("mom", "en"), 0, 0)
    result = jnp.swapaxes(back, 0, 1).reshape(pairs.shape)
    return result[None]


def solution(mesh):
    placed = (
        P("mom", "en", None, None, None, None),
        P("mom", None, None, None, None),
        P("mom", "en", None, None),
        P(),
        P(),
        P("mom", None),
        P(),
        P(),
    )
    return jax.shard_map(
        shards,
        mesh=mesh,
        in_specs=placed,
        out_specs=P("mom", "en", None, None, None),
        check_vma=False,
    )
```

```python
import jax
import jax.numpy as jnp
from jax import lax
from jax.sharding import PartitionSpec as P

SHIFT_MAX = 2
OFFSETS = (-2, -1, 1, 2)


HIGH = lax.Precision.HIGHEST


def with_halo(x, sides, width):
    for axis, dim in sides:
        count, length = (lax.axis_size(axis), x.shape[dim])
        up = [(i, (i + 1) % count) for i in range(count - 1)]
        down = [(j, i) for i, j in up]
        last = lax.slice_in_dim(x, length - width, length, axis=dim)
        leading = lax.slice_in_dim(x, 0, width, axis=dim)
        before = lax.ppermute(last, axis, up)
        after = lax.ppermute(leading, axis, down)
        x = jnp.concatenate([before, x, after], axis=dim)
    return x


def block(value):
    real, imag = value[..., 0, :, :], value[..., 1, :, :]
    top = jnp.concatenate([real, -imag], axis=-1)
    bottom = jnp.concatenate([imag, real], axis=-1)
    return jnp.concatenate([top, bottom], axis=-2)


def column(value, adjoint=False):
    real, imag = value[..., 0, :, :], value[..., 1, :, :]
    if adjoint:
        real, imag = jnp.swapaxes(real, -1, -2), -jnp.swapaxes(imag, -1, -2)
    return jnp.concatenate([real, imag], axis=-2)


def split(value):
    rows = value.shape[-2] // 2
    return value.reshape(value.shape[:-2] + (2, rows, value.shape[-1]))


def cmul(left, right, spec="...ij,...jk->...ik", adjoint=False):
    product = jnp.einsum(spec, block(left), column(right, adjoint), precision=HIGH)
    return split(product)


def slab_pairs(slab_inverse, coupling, injection, neighbors):
    orbitals = slab_inverse.shape[-1]
    slab_count = slab_inverse.shape[1]
    eye = jnp.eye(orbitals, dtype=jnp.float32)
    retarded = slab_inverse[:, 0]
    source = injection[:, 0][:, None, None, :]
    lesser = cmul(retarded * source, retarded, adjoint=True)
    collected = [lesser]
    for slab in range(1, slab_count):
        inverse = slab_inverse[:, slab]
        link = coupling[slab]
        both = jnp.concatenate([retarded, lesser], axis=-1)
        linked = cmul(link, both, "ij,ejk->eik")
        linked = jnp.stack([linked[..., :orbitals], linked[..., orbitals:]], axis=1)
        sandwich = cmul(linked, link, "ewij,jk->ewik", adjoint=True)
        sigma, middle = sandwich[:, 0], sandwich[:, 1]
        diagonal = eye[None] * injection[:, slab][:, None, :]
        middle = jnp.stack([middle[:, 0] + diagonal, middle[:, 1]], axis=1)
        inner = cmul(cmul(inverse, sigma), inverse)
        retarded = inverse + inner
        lesser = cmul(cmul(retarded, middle), retarded, adjoint=True)
        collected.append(lesser)
    stacked = jnp.stack(collected, axis=1)
    pieces = []
    rest = stacked
    for _ in range(3):
        piece = rest.astype(jnp.bfloat16)
        pieces.append(piece)
        rest = rest - piece.astype(jnp.float32)
    columns = jnp.arange(orbitals, dtype=jnp.int32)
    selector = (neighbors[..., None] == columns).astype(jnp.bfloat16)
    picked = jnp.einsum(
        "qesxoc,sojc->qesjxo", jnp.stack(pieces), selector, preferred_element_type=jnp.float32
    )
    picked = picked[0] + picked[1] + picked[2]
    return picked.reshape(picked.shape[0], -1, picked.shape[3], picked.shape[4])


def shift_weights(table_row, mode_shift, emit_weight, absorb_weight):
    mode_ids = jnp.arange(mode_shift.shape[0], dtype=jnp.int32)
    chosen = (table_row[:, None] == mode_ids[None, :]).astype(jnp.float32)
    shift = jnp.sum(chosen * mode_shift.astype(jnp.float32)[None], axis=1)
    emit = jnp.sum(chosen * emit_weight[None], axis=1)
    absorb = jnp.sum(chosen * absorb_weight[None], axis=1)
    rows = []
    for offset in OFFSETS:
        if offset < 0:
            rows.append(emit * (shift == -offset).astype(jnp.float32))
        else:
            rows.append(absorb * (shift == offset).astype(jnp.float32))
    return jnp.stack(rows) / table_row.shape[0]


def mix(data, weights, energies):
    total = None
    for index, offset in enumerate(OFFSETS):
        window = data[:, SHIFT_MAX + offset : SHIFT_MAX + offset + energies]
        term = jnp.einsum("kj,jec->kec", weights[:, index], window, precision=HIGH)
        total = term if total is None else total + term
    return total


def shards(
    slab_inverse, coupling, injection, neighbors, mode_shift, mode_table, emit_weight, absorb_weight
):
    pairs = slab_pairs(slab_inverse[0], coupling[0], injection[0], neighbors)
    local = pairs.shape[0]
    moms, groups = lax.axis_size("mom"), lax.axis_size("en")
    devices = moms * groups
    flat = pairs.reshape(local, -1)
    width = flat.shape[1] // devices
    blocks = jnp.swapaxes(flat.reshape(local, devices, width), 0, 1)
    weights = shift_weights(mode_table[0], mode_shift, emit_weight, absorb_weight).reshape(-1)
    share = -(-weights.shape[0] // (groups * width)) * width
    weights = jnp.pad(weights, (0, share * groups - weights.shape[0]))
    mine = lax.dynamic_slice_in_dim(weights, lax.axis_index("en") * share, share)
    rows = jnp.broadcast_to(mine.reshape(1, -1, width), (devices, share // width, width))
    sent = lax.all_to_all(jnp.concatenate([blocks, rows], axis=1), ("mom", "en"), 0, 0)
    sent = sent.reshape(moms, groups, local + share // width, width)
    data = sent[:, :, :local].reshape(moms, groups * local, width)
    data = jnp.pad(data, ((0, 0), (SHIFT_MAX, SHIFT_MAX), (0, 0)))
    table = sent[:, :, local:].reshape(moms, -1)[:, : len(OFFSETS) * moms]
    mixed = mix(data, table.reshape(moms, len(OFFSETS), moms), groups * local)
    mixed = mixed.reshape(devices, local, width)
    back = lax.all_to_all(mixed, ("mom", "en"), 0, 0)
    result = jnp.swapaxes(back, 0, 1).reshape(pairs.shape)
    return result[None]


def solution(mesh):
    placed = (
        P("mom", "en", None, None, None, None),
        P("mom", None, None, None, None),
        P("mom", "en", None, None),
        P(),
        P(),
        P("mom", None),
        P(),
        P(),
    )
    return jax.shard_map(
        shards,
        mesh=mesh,
        in_specs=placed,
        out_specs=P("mom", "en", None, None, None),
        check_vma=False,
    )
```

```python
import jax
import jax.numpy as jnp
from jax import lax
from jax.sharding import PartitionSpec as P

SHIFT_MAX = 2
OFFSETS = (-2, -1, 1, 2)


HIGH = lax.Precision.HIGHEST


def with_halo(x, sides, width):
    for axis, dim in sides:
        count, length = (lax.axis_size(axis), x.shape[dim])
        up = [(i, (i + 1) % count) for i in range(count - 1)]
        down = [(j, i) for i, j in up]
        last = lax.slice_in_dim(x, length - width, length, axis=dim)
        leading = lax.slice_in_dim(x, 0, width, axis=dim)
        before = lax.ppermute(last, axis, up)
        after = lax.ppermute(leading, axis, down)
        x = jnp.concatenate([before, x, after], axis=dim)
    return x


def block(value):
    real, imag = value[..., 0, :, :], value[..., 1, :, :]
    top = jnp.concatenate([real, -imag], axis=-1)
    bottom = jnp.concatenate([imag, real], axis=-1)
    return jnp.concatenate([top, bottom], axis=-2)


def column(value, adjoint=False):
    real, imag = value[..., 0, :, :], value[..., 1, :, :]
    if adjoint:
        real, imag = jnp.swapaxes(real, -1, -2), -jnp.swapaxes(imag, -1, -2)
    return jnp.concatenate([real, imag], axis=-2)


def split(value):
    rows = value.shape[-2] // 2
    return value.reshape(value.shape[:-2] + (2, rows, value.shape[-1]))


def cmul(left, right, spec="...ij,...jk->...ik", adjoint=False):
    product = jnp.einsum(spec, block(left), column(right, adjoint), precision=HIGH)
    return split(product)


def slab_pairs(slab_inverse, coupling, injection, neighbors):
    orbitals = slab_inverse.shape[-1]
    slab_count = slab_inverse.shape[1]
    eye = jnp.eye(orbitals, dtype=jnp.float32)
    retarded = slab_inverse[:, 0]
    source = injection[:, 0][:, None, None, :]
    lesser = cmul(retarded * source, retarded, adjoint=True)
    collected = [lesser]
    for slab in range(1, slab_count):
        inverse = slab_inverse[:, slab]
        link = coupling[slab]
        both = jnp.concatenate([retarded, lesser], axis=-1)
        linked = cmul(link, both, "ij,ejk->eik")
        linked = jnp.stack([linked[..., :orbitals], linked[..., orbitals:]], axis=1)
        sandwich = cmul(linked, link, "ewij,jk->ewik", adjoint=True)
        sigma, middle = sandwich[:, 0], sandwich[:, 1]
        diagonal = eye[None] * injection[:, slab][:, None, :]
        middle = jnp.stack([middle[:, 0] + diagonal, middle[:, 1]], axis=1)
        inner = cmul(cmul(inverse, sigma), inverse)
        retarded = inverse + inner
        lesser = cmul(cmul(retarded, middle), retarded, adjoint=True)
        collected.append(lesser)
    stacked = jnp.stack(collected, axis=1)
    pieces = []
    rest = stacked
    for _ in range(3):
        piece = lax.reduce_precision(rest, exponent_bits=8, mantissa_bits=7)
        pieces.append(piece.astype(jnp.bfloat16))
        rest = rest - piece
    columns = jnp.arange(orbitals, dtype=jnp.int32)
    selector = (neighbors[..., None] == columns).astype(jnp.bfloat16)
    picked = jnp.einsum(
        "qesxoc,sojc->qesjxo", jnp.stack(pieces), selector, preferred_element_type=jnp.float32
    )
    picked = picked[0] + picked[1] + picked[2]
    return picked.reshape(picked.shape[0], -1, picked.shape[3], picked.shape[4])


def shift_weights(table_row, mode_shift, emit_weight, absorb_weight):
    mode_ids = jnp.arange(mode_shift.shape[0], dtype=jnp.int32)
    chosen = (table_row[:, None] == mode_ids[None, :]).astype(jnp.float32)
    shift = jnp.sum(chosen * mode_shift.astype(jnp.float32)[None], axis=1)
    emit = jnp.sum(chosen * emit_weight[None], axis=1)
    absorb = jnp.sum(chosen * absorb_weight[None], axis=1)
    rows = []
    for offset in OFFSETS:
        if offset < 0:
            rows.append(emit * (shift == -offset).astype(jnp.float32))
        else:
            rows.append(absorb * (shift == offset).astype(jnp.float32))
    return jnp.stack(rows) / table_row.shape[0]


def mix(data, weights, energies):
    total = None
    for index, offset in enumerate(OFFSETS):
        window = data[:, SHIFT_MAX + offset : SHIFT_MAX + offset + energies]
        term = jnp.einsum("kj,jec->kec", weights[:, index], window, precision=HIGH)
        total = term if total is None else total + term
    return total


def shards(
    slab_inverse, coupling, injection, neighbors, mode_shift, mode_table, emit_weight, absorb_weight
):
    pairs = slab_pairs(slab_inverse[0], coupling[0], injection[0], neighbors)
    local = pairs.shape[0]
    moms, groups = lax.axis_size("mom"), lax.axis_size("en")
    devices = moms * groups
    flat = pairs.reshape(local, -1)
    width = flat.shape[1] // devices
    blocks = jnp.swapaxes(flat.reshape(local, devices, width), 0, 1)
    weights = shift_weights(mode_table[0], mode_shift, emit_weight, absorb_weight).reshape(-1)
    share = -(-weights.shape[0] // (groups * width)) * width
    weights = jnp.pad(weights, (0, share * groups - weights.shape[0]))
    mine = lax.dynamic_slice_in_dim(weights, lax.axis_index("en") * share, share)
    rows = jnp.broadcast_to(mine.reshape(1, -1, width), (devices, share // width, width))
    sent = lax.all_to_all(jnp.concatenate([blocks, rows], axis=1), ("mom", "en"), 0, 0)
    sent = sent.reshape(moms, groups, local + share // width, width)
    data = sent[:, :, :local].reshape(moms, groups * local, width)
    data = jnp.pad(data, ((0, 0), (SHIFT_MAX, SHIFT_MAX), (0, 0)))
    table = sent[:, :, local:].reshape(moms, -1)[:, : len(OFFSETS) * moms]
    mixed = mix(data, table.reshape(moms, len(OFFSETS), moms), groups * local)
    mixed = mixed.reshape(devices, local, width)
    back = lax.all_to_all(mixed, ("mom", "en"), 0, 0)
    result = jnp.swapaxes(back, 0, 1).reshape(pairs.shape)
    return result[None]


def solution(mesh):
    placed = (
        P("mom", "en", None, None, None, None),
        P("mom", None, None, None, None),
        P("mom", "en", None, None),
        P(),
        P(),
        P("mom", None),
        P(),
        P(),
    )
    return jax.shard_map(
        shards,
        mesh=mesh,
        in_specs=placed,
        out_specs=P("mom", "en", None, None, None),
        check_vma=False,
    )
```

```python
import jax
import jax.numpy as jnp
from jax import lax
from jax.sharding import PartitionSpec as P

SHIFT_MAX = 2
OFFSETS = (-2, -1, 1, 2)


HIGH = lax.Precision.HIGHEST


def with_halo(x, sides, width):
    for axis, dim in sides:
        count, length = (lax.axis_size(axis), x.shape[dim])
        up = [(i, (i + 1) % count) for i in range(count - 1)]
        down = [(j, i) for i, j in up]
        last = lax.slice_in_dim(x, length - width, length, axis=dim)
        leading = lax.slice_in_dim(x, 0, width, axis=dim)
        before = lax.ppermute(last, axis, up)
        after = lax.ppermute(leading, axis, down)
        x = jnp.concatenate([before, x, after], axis=dim)
    return x


def block(value):
    real, imag = value[..., 0, :, :], value[..., 1, :, :]
    top = jnp.concatenate([real, -imag], axis=-1)
    bottom = jnp.concatenate([imag, real], axis=-1)
    return jnp.concatenate([top, bottom], axis=-2)


def column(value, adjoint=False):
    real, imag = value[..., 0, :, :], value[..., 1, :, :]
    if adjoint:
        real, imag = jnp.swapaxes(real, -1, -2), -jnp.swapaxes(imag, -1, -2)
    return jnp.concatenate([real, imag], axis=-2)


def split(value):
    rows = value.shape[-2] // 2
    return value.reshape(value.shape[:-2] + (2, rows, value.shape[-1]))


def cmul(left, right, spec="...ij,...jk->...ik", adjoint=False):
    product = jnp.einsum(spec, block(left), column(right, adjoint), precision=HIGH)
    return split(product)


def slab_pairs(slab_inverse, coupling, injection, neighbors):
    orbitals = slab_inverse.shape[-1]
    slab_count = slab_inverse.shape[1]
    eye = jnp.eye(orbitals, dtype=jnp.float32)
    retarded = slab_inverse[:, 0]
    source = injection[:, 0][:, None, None, :]
    lesser = cmul(retarded * source, retarded, adjoint=True)
    collected = [lesser]
    for slab in range(1, slab_count):
        inverse = slab_inverse[:, slab]
        link = coupling[slab]
        both = jnp.concatenate([retarded, lesser], axis=-1)
        linked = cmul(link, both, "ij,ejk->eik")
        linked = jnp.stack([linked[..., :orbitals], linked[..., orbitals:]], axis=1)
        sandwich = cmul(linked, link, "ewij,jk->ewik", adjoint=True)
        sigma, middle = sandwich[:, 0], sandwich[:, 1]
        diagonal = eye[None] * injection[:, slab][:, None, :]
        middle = jnp.stack([middle[:, 0] + diagonal, middle[:, 1]], axis=1)
        inner = cmul(cmul(inverse, sigma), inverse)
        retarded = inverse + inner
        lesser = cmul(cmul(retarded, middle), retarded, adjoint=True)
        collected.append(lesser)
    stacked = jnp.stack(collected, axis=1)
    pieces = []
    rest = stacked
    for _ in range(3):
        piece = lax.reduce_precision(rest, exponent_bits=8, mantissa_bits=7)
        pieces.append(piece.astype(jnp.bfloat16))
        rest = rest - piece
    columns = jnp.arange(orbitals, dtype=jnp.int32)
    selector = (neighbors[..., None] == columns).astype(jnp.bfloat16)
    picked = jnp.einsum(
        "qesxoc,sojc->qesjxo", jnp.stack(pieces), selector, preferred_element_type=jnp.float32
    )
    picked = picked[0] + picked[1] + picked[2]
    return picked.reshape(picked.shape[0], -1, picked.shape[3], picked.shape[4])


def shift_weights(table, mode_shift, emit_weight, absorb_weight):
    mode_ids = jnp.arange(mode_shift.shape[0], dtype=jnp.int32)
    chosen = (table[..., None] == mode_ids).astype(jnp.float32)
    shift = jnp.sum(chosen * mode_shift.astype(jnp.float32), axis=-1)
    emit = jnp.sum(chosen * emit_weight, axis=-1)
    absorb = jnp.sum(chosen * absorb_weight, axis=-1)
    rows = []
    for offset in OFFSETS:
        if offset < 0:
            rows.append(emit * (shift == -offset).astype(jnp.float32))
        else:
            rows.append(absorb * (shift == offset).astype(jnp.float32))
    return jnp.stack(rows, axis=-2) / table.shape[-1]


def mix(data, weights, energies):
    total = None
    for index, offset in enumerate(OFFSETS):
        window = data[:, SHIFT_MAX + offset : SHIFT_MAX + offset + energies]
        term = jnp.einsum("kj,jec->kec", weights[:, index], window, precision=HIGH)
        total = term if total is None else total + term
    return total


def shards(
    slab_inverse, coupling, injection, neighbors, mode_shift, mode_table, emit_weight, absorb_weight
):
    pairs = slab_pairs(slab_inverse[0], coupling[0], injection[0], neighbors)
    local = pairs.shape[0]
    moms, groups = lax.axis_size("mom"), lax.axis_size("en")
    devices = moms * groups
    flat = pairs.reshape(local, -1)
    width = flat.shape[1] // devices
    blocks = jnp.swapaxes(flat.reshape(local, devices, width), 0, 1).reshape(devices, -1)
    share = -(-moms // groups)
    ids = jnp.pad(mode_table[0].astype(jnp.float32), (0, share * groups - moms))
    mine = lax.dynamic_slice_in_dim(ids, lax.axis_index("en") * share, share)
    rows = jnp.broadcast_to(mine[None], (devices, share))
    sent = lax.all_to_all(jnp.concatenate([blocks, rows], axis=1), ("mom", "en"), 0, 0)
    sent = sent.reshape(moms, groups, -1)
    data = sent[:, :, : local * width].reshape(moms, groups * local, width)
    data = jnp.pad(data, ((0, 0), (SHIFT_MAX, SHIFT_MAX), (0, 0)))
    table = sent[:, :, local * width :].reshape(moms, -1)[:, :moms].astype(jnp.int32)
    weights = shift_weights(table, mode_shift, emit_weight, absorb_weight)
    mixed = mix(data, weights, groups * local)
    mixed = mixed.reshape(devices, local, width)
    back = lax.all_to_all(mixed, ("mom", "en"), 0, 0)
    result = jnp.swapaxes(back, 0, 1).reshape(pairs.shape)
    return result[None]


def solution(mesh):
    placed = (
        P("mom", "en", None, None, None, None),
        P("mom", None, None, None, None),
        P("mom", "en", None, None),
        P(),
        P(),
        P("mom", None),
        P(),
        P(),
    )
    return jax.shard_map(
        shards,
        mesh=mesh,
        in_specs=placed,
        out_specs=P("mom", "en", None, None, None),
        check_vma=False,
    )
```

```python
import jax
import jax.numpy as jnp
from jax import lax
from jax.sharding import PartitionSpec as P

SHIFT_MAX = 2
OFFSETS = (-2, -1, 1, 2)


HIGH = lax.Precision.HIGHEST
CHAIN = lax.Precision.HIGH


def with_halo(x, sides, width):
    for axis, dim in sides:
        count, length = (lax.axis_size(axis), x.shape[dim])
        up = [(i, (i + 1) % count) for i in range(count - 1)]
        down = [(j, i) for i, j in up]
        last = lax.slice_in_dim(x, length - width, length, axis=dim)
        leading = lax.slice_in_dim(x, 0, width, axis=dim)
        before = lax.ppermute(last, axis, up)
        after = lax.ppermute(leading, axis, down)
        x = jnp.concatenate([before, x, after], axis=dim)
    return x


def block(value):
    real, imag = value[..., 0, :, :], value[..., 1, :, :]
    top = jnp.concatenate([real, -imag], axis=-1)
    bottom = jnp.concatenate([imag, real], axis=-1)
    return jnp.concatenate([top, bottom], axis=-2)


def column(value, adjoint=False):
    real, imag = value[..., 0, :, :], value[..., 1, :, :]
    if adjoint:
        real, imag = jnp.swapaxes(real, -1, -2), -jnp.swapaxes(imag, -1, -2)
    return jnp.concatenate([real, imag], axis=-2)


def split(value):
    rows = value.shape[-2] // 2
    return value.reshape(value.shape[:-2] + (2, rows, value.shape[-1]))


def cmul(left, right, spec="...ij,...jk->...ik", adjoint=False):
    product = jnp.einsum(spec, block(left), column(right, adjoint), precision=CHAIN)
    return split(product)


def slab_pairs(slab_inverse, coupling, injection, neighbors):
    orbitals = slab_inverse.shape[-1]
    slab_count = slab_inverse.shape[1]
    eye = jnp.eye(orbitals, dtype=jnp.float32)
    retarded = slab_inverse[:, 0]
    source = injection[:, 0][:, None, None, :]
    lesser = cmul(retarded * source, retarded, adjoint=True)
    collected = [lesser]
    for slab in range(1, slab_count):
        inverse = slab_inverse[:, slab]
        link = coupling[slab]
        both = jnp.concatenate([retarded, lesser], axis=-1)
        linked = cmul(link, both, "ij,ejk->eik")
        linked = jnp.stack([linked[..., :orbitals], linked[..., orbitals:]], axis=1)
        sandwich = cmul(linked, link, "ewij,jk->ewik", adjoint=True)
        sigma, middle = sandwich[:, 0], sandwich[:, 1]
        diagonal = eye[None] * injection[:, slab][:, None, :]
        middle = jnp.stack([middle[:, 0] + diagonal, middle[:, 1]], axis=1)
        inner = cmul(cmul(inverse, sigma), inverse)
        retarded = inverse + inner
        lesser = cmul(cmul(retarded, middle), retarded, adjoint=True)
        collected.append(lesser)
    stacked = jnp.stack(collected, axis=1)
    pieces = []
    rest = stacked
    for _ in range(3):
        piece = lax.reduce_precision(rest, exponent_bits=8, mantissa_bits=7)
        pieces.append(piece.astype(jnp.bfloat16))
        rest = rest - piece
    columns = jnp.arange(orbitals, dtype=jnp.int32)
    selector = (neighbors[..., None] == columns).astype(jnp.bfloat16)
    picked = jnp.einsum(
        "qesxoc,sojc->qesjxo", jnp.stack(pieces), selector, preferred_element_type=jnp.float32
    )
    picked = picked[0] + picked[1] + picked[2]
    return picked.reshape(picked.shape[0], -1, picked.shape[3], picked.shape[4])


def shift_weights(table, mode_shift, emit_weight, absorb_weight):
    mode_ids = jnp.arange(mode_shift.shape[0], dtype=jnp.int32)
    chosen = (table[..., None] == mode_ids).astype(jnp.float32)
    shift = jnp.sum(chosen * mode_shift.astype(jnp.float32), axis=-1)
    emit = jnp.sum(chosen * emit_weight, axis=-1)
    absorb = jnp.sum(chosen * absorb_weight, axis=-1)
    rows = []
    for offset in OFFSETS:
        if offset < 0:
            rows.append(emit * (shift == -offset).astype(jnp.float32))
        else:
            rows.append(absorb * (shift == offset).astype(jnp.float32))
    return jnp.stack(rows, axis=-2) / table.shape[-1]


def mix(data, weights, energies):
    total = None
    for index, offset in enumerate(OFFSETS):
        window = data[:, SHIFT_MAX + offset : SHIFT_MAX + offset + energies]
        term = jnp.einsum("kj,jec->kec", weights[:, index], window, precision=HIGH)
        total = term if total is None else total + term
    return total


def shards(
    slab_inverse, coupling, injection, neighbors, mode_shift, mode_table, emit_weight, absorb_weight
):
    pairs = slab_pairs(slab_inverse[0], coupling[0], injection[0], neighbors)
    local = pairs.shape[0]
    moms, groups = lax.axis_size("mom"), lax.axis_size("en")
    devices = moms * groups
    flat = pairs.reshape(local, -1)
    width = flat.shape[1] // devices
    blocks = jnp.swapaxes(flat.reshape(local, devices, width), 0, 1).reshape(devices, -1)
    share = -(-moms // groups)
    ids = jnp.pad(mode_table[0].astype(jnp.float32), (0, share * groups - moms))
    mine = lax.dynamic_slice_in_dim(ids, lax.axis_index("en") * share, share)
    rows = jnp.broadcast_to(mine[None], (devices, share))
    sent = lax.all_to_all(jnp.concatenate([blocks, rows], axis=1), ("mom", "en"), 0, 0)
    sent = sent.reshape(moms, groups, -1)
    data = sent[:, :, : local * width].reshape(moms, groups * local, width)
    data = jnp.pad(data, ((0, 0), (SHIFT_MAX, SHIFT_MAX), (0, 0)))
    table = sent[:, :, local * width :].reshape(moms, -1)[:, :moms].astype(jnp.int32)
    weights = shift_weights(table, mode_shift, emit_weight, absorb_weight)
    mixed = mix(data, weights, groups * local)
    mixed = mixed.reshape(devices, local, width)
    back = lax.all_to_all(mixed, ("mom", "en"), 0, 0)
    result = jnp.swapaxes(back, 0, 1).reshape(pairs.shape)
    return result[None]


def solution(mesh):
    placed = (
        P("mom", "en", None, None, None, None),
        P("mom", None, None, None, None),
        P("mom", "en", None, None),
        P(),
        P(),
        P("mom", None),
        P(),
        P(),
    )
    return jax.shard_map(
        shards,
        mesh=mesh,
        in_specs=placed,
        out_specs=P("mom", "en", None, None, None),
        check_vma=False,
    )
```

```python
import jax
import jax.numpy as jnp
from jax import lax
from jax.sharding import PartitionSpec as P

SHIFT_MAX = 2
OFFSETS = (-2, -1, 1, 2)


HIGH = lax.Precision.HIGHEST
CHAIN = lax.Precision.HIGH


def with_halo(x, sides, width):
    for axis, dim in sides:
        count, length = (lax.axis_size(axis), x.shape[dim])
        up = [(i, (i + 1) % count) for i in range(count - 1)]
        down = [(j, i) for i, j in up]
        last = lax.slice_in_dim(x, length - width, length, axis=dim)
        leading = lax.slice_in_dim(x, 0, width, axis=dim)
        before = lax.ppermute(last, axis, up)
        after = lax.ppermute(leading, axis, down)
        x = jnp.concatenate([before, x, after], axis=dim)
    return x


def block(value):
    real, imag = value[..., 0, :, :], value[..., 1, :, :]
    top = jnp.concatenate([real, -imag], axis=-1)
    bottom = jnp.concatenate([imag, real], axis=-1)
    return jnp.concatenate([top, bottom], axis=-2)


def column(value, adjoint=False):
    real, imag = value[..., 0, :, :], value[..., 1, :, :]
    if adjoint:
        real, imag = jnp.swapaxes(real, -1, -2), -jnp.swapaxes(imag, -1, -2)
    return jnp.concatenate([real, imag], axis=-2)


def split(value):
    rows = value.shape[-2] // 2
    return value.reshape(value.shape[:-2] + (2, rows, value.shape[-1]))


def cmul(left, right, spec="...ij,...jk->...ik", adjoint=False):
    product = jnp.einsum(spec, block(left), column(right, adjoint), precision=CHAIN)
    return split(product)


def slab_pairs(slab_inverse, coupling, injection, neighbors):
    orbitals = slab_inverse.shape[-1]
    slab_count = slab_inverse.shape[1]
    eye = jnp.eye(orbitals, dtype=jnp.float32)
    retarded = slab_inverse[:, 0]
    source = injection[:, 0][:, None, None, :]
    lesser = cmul(retarded * source, retarded, adjoint=True)
    collected = [lesser]
    for slab in range(1, slab_count):
        inverse = slab_inverse[:, slab]
        link = coupling[slab]
        both = jnp.concatenate([retarded, lesser], axis=-1)
        linked = cmul(link, both, "ij,ejk->eik")
        linked = jnp.stack([linked[..., :orbitals], linked[..., orbitals:]], axis=1)
        sandwich = cmul(linked, link, "ewij,jk->ewik", adjoint=True)
        sigma, middle = sandwich[:, 0], sandwich[:, 1]
        diagonal = eye[None] * injection[:, slab][:, None, :]
        middle = jnp.stack([middle[:, 0] + diagonal, middle[:, 1]], axis=1)
        inner = cmul(cmul(inverse, sigma), inverse)
        retarded = inverse + inner
        lesser = cmul(cmul(retarded, middle), retarded, adjoint=True)
        collected.append(lesser)
    stacked = jnp.stack(collected, axis=1)
    pieces = []
    rest = stacked
    for _ in range(3):
        piece = lax.reduce_precision(rest, exponent_bits=8, mantissa_bits=7)
        pieces.append(piece.astype(jnp.bfloat16))
        rest = rest - piece
    columns = jnp.arange(orbitals, dtype=jnp.int32)
    selector = (neighbors[..., None] == columns).astype(jnp.bfloat16)
    picked = jnp.einsum(
        "qesxoc,sojc->qesjxo", jnp.stack(pieces), selector, preferred_element_type=jnp.float32
    )
    picked = picked[0] + picked[1] + picked[2]
    return picked.reshape(picked.shape[0], -1, picked.shape[3], picked.shape[4])


def shift_weights(table, mode_shift, emit_weight, absorb_weight):
    mode_ids = jnp.arange(mode_shift.shape[0], dtype=jnp.int32)
    chosen = (table[..., None] == mode_ids).astype(jnp.float32)
    shift = jnp.sum(chosen * mode_shift.astype(jnp.float32), axis=-1)
    emit = jnp.sum(chosen * emit_weight, axis=-1)
    absorb = jnp.sum(chosen * absorb_weight, axis=-1)
    rows = []
    for offset in OFFSETS:
        if offset < 0:
            rows.append(emit * (shift == -offset).astype(jnp.float32))
        else:
            rows.append(absorb * (shift == offset).astype(jnp.float32))
    return jnp.stack(rows, axis=-2) / table.shape[-1]


def mix(data, weights, energies):
    total = None
    for index, offset in enumerate(OFFSETS):
        window = data[:, SHIFT_MAX + offset : SHIFT_MAX + offset + energies]
        term = jnp.einsum("kj,jec->kec", weights[:, index], window, precision=HIGH)
        total = term if total is None else total + term
    return total


def gather_rows(rows, axis):
    count, index = lax.axis_size(axis), lax.axis_index(axis)
    step = 1
    while step < count:
        pairs = [(i, i ^ step) for i in range(count)]
        other = lax.ppermute(rows, axis, pairs)
        low = (index // step) % 2 == 0
        rows = jnp.where(low, jnp.concatenate([rows, other]), jnp.concatenate([other, rows]))
        step *= 2
    return rows


def shards(
    slab_inverse, coupling, injection, neighbors, mode_shift, mode_table, emit_weight, absorb_weight
):
    pairs = slab_pairs(slab_inverse[0], coupling[0], injection[0], neighbors)
    local = pairs.shape[0]
    moms, groups = lax.axis_size("mom"), lax.axis_size("en")
    devices = moms * groups
    flat = pairs.reshape(local, -1)
    width = flat.shape[1] // devices
    blocks = jnp.swapaxes(flat.reshape(local, devices, width), 0, 1)
    table = gather_rows(mode_table[0].astype(jnp.float32)[None], "mom").astype(jnp.int32)
    sent = lax.all_to_all(blocks, ("mom", "en"), 0, 0)
    data = sent.reshape(moms, groups * local, width)
    data = jnp.pad(data, ((0, 0), (SHIFT_MAX, SHIFT_MAX), (0, 0)))
    weights = shift_weights(table, mode_shift, emit_weight, absorb_weight)
    mixed = mix(data, weights, groups * local)
    mixed = mixed.reshape(devices, local, width)
    back = lax.all_to_all(mixed, ("mom", "en"), 0, 0)
    result = jnp.swapaxes(back, 0, 1).reshape(pairs.shape)
    return result[None]


def solution(mesh):
    placed = (
        P("mom", "en", None, None, None, None),
        P("mom", None, None, None, None),
        P("mom", "en", None, None),
        P(),
        P(),
        P("mom", None),
        P(),
        P(),
    )
    return jax.shard_map(
        shards,
        mesh=mesh,
        in_specs=placed,
        out_specs=P("mom", "en", None, None, None),
        check_vma=False,
    )
```

```python
import jax
import jax.numpy as jnp
from jax import lax
from jax.sharding import PartitionSpec as P

SHIFT_MAX = 2
OFFSETS = (-2, -1, 1, 2)


HIGH = lax.Precision.HIGHEST
CHAIN = lax.Precision.HIGH


def with_halo(x, sides, width):
    for axis, dim in sides:
        count, length = (lax.axis_size(axis), x.shape[dim])
        up = [(i, (i + 1) % count) for i in range(count - 1)]
        down = [(j, i) for i, j in up]
        last = lax.slice_in_dim(x, length - width, length, axis=dim)
        leading = lax.slice_in_dim(x, 0, width, axis=dim)
        before = lax.ppermute(last, axis, up)
        after = lax.ppermute(leading, axis, down)
        x = jnp.concatenate([before, x, after], axis=dim)
    return x


def block(value):
    real, imag = value[..., 0, :, :], value[..., 1, :, :]
    top = jnp.concatenate([real, -imag], axis=-1)
    bottom = jnp.concatenate([imag, real], axis=-1)
    return jnp.concatenate([top, bottom], axis=-2)


def column(value, adjoint=False):
    real, imag = value[..., 0, :, :], value[..., 1, :, :]
    if adjoint:
        real, imag = jnp.swapaxes(real, -1, -2), -jnp.swapaxes(imag, -1, -2)
    return jnp.concatenate([real, imag], axis=-2)


def split(value):
    rows = value.shape[-2] // 2
    return value.reshape(value.shape[:-2] + (2, rows, value.shape[-1]))


def cmul(left, right, spec="...ij,...jk->...ik", adjoint=False):
    product = jnp.einsum(spec, block(left), column(right, adjoint), precision=CHAIN)
    return split(product)


def slab_pairs(slab_inverse, coupling, injection, neighbors):
    orbitals = slab_inverse.shape[-1]
    slab_count = slab_inverse.shape[1]
    eye = jnp.eye(orbitals, dtype=jnp.float32)
    retarded = slab_inverse[:, 0]
    source = injection[:, 0][:, None, None, :]
    lesser = cmul(retarded * source, retarded, adjoint=True)
    collected = [lesser]
    for slab in range(1, slab_count):
        inverse = slab_inverse[:, slab]
        link = coupling[slab]
        both = jnp.concatenate([retarded, lesser], axis=-1)
        linked = cmul(link, both, "ij,ejk->eik")
        linked = jnp.stack([linked[..., :orbitals], linked[..., orbitals:]], axis=1)
        sandwich = cmul(linked, link, "ewij,jk->ewik", adjoint=True)
        sigma, middle = sandwich[:, 0], sandwich[:, 1]
        diagonal = eye[None] * injection[:, slab][:, None, :]
        middle = jnp.stack([middle[:, 0] + diagonal, middle[:, 1]], axis=1)
        inner = cmul(cmul(inverse, sigma), inverse)
        retarded = inverse + inner
        lesser = cmul(cmul(retarded, middle), retarded, adjoint=True)
        collected.append(lesser)
    stacked = jnp.stack(collected, axis=1)
    pieces = []
    rest = stacked
    for _ in range(3):
        piece = lax.reduce_precision(rest, exponent_bits=8, mantissa_bits=7)
        pieces.append(piece.astype(jnp.bfloat16))
        rest = rest - piece
    columns = jnp.arange(orbitals, dtype=jnp.int32)
    selector = (neighbors[..., None] == columns).astype(jnp.bfloat16)
    picked = jnp.einsum(
        "qesxoc,sojc->qesjxo", jnp.stack(pieces), selector, preferred_element_type=jnp.float32
    )
    picked = picked[0] + picked[1] + picked[2]
    return picked.reshape(picked.shape[0], -1, picked.shape[3], picked.shape[4])


def shift_weights(table, mode_shift, emit_weight, absorb_weight):
    mode_ids = jnp.arange(mode_shift.shape[0], dtype=jnp.int32)
    chosen = (table[..., None] == mode_ids).astype(jnp.float32)
    shift = jnp.sum(chosen * mode_shift.astype(jnp.float32), axis=-1)
    emit = jnp.sum(chosen * emit_weight, axis=-1)
    absorb = jnp.sum(chosen * absorb_weight, axis=-1)
    rows = []
    for offset in OFFSETS:
        if offset < 0:
            rows.append(emit * (shift == -offset).astype(jnp.float32))
        else:
            rows.append(absorb * (shift == offset).astype(jnp.float32))
    return jnp.stack(rows, axis=-2) / table.shape[-1]


def mix(data, weights, energies):
    total = None
    for index, offset in enumerate(OFFSETS):
        window = data[:, SHIFT_MAX + offset : SHIFT_MAX + offset + energies]
        term = jnp.einsum("kj,jec->kec", weights[:, index], window, precision=HIGH)
        total = term if total is None else total + term
    return total


def gather_rows(rows, axis, group=8):
    count, index = lax.axis_size(axis), lax.axis_index(axis)
    stride = 1
    while stride < count:
        size = min(group, count // stride)
        position = (index // stride) % size
        received = [rows]
        for shift in range(1, size):
            pairs = []
            for i in range(count):
                low = (i // stride) % size
                target = i + (((low + shift) % size) - low) * stride
                pairs.append((i, target))
            received.append(lax.ppermute(rows, axis, pairs))
        stacked = jnp.stack(received)
        slots = (position - jnp.arange(size)) % size
        order = (slots[:, None] == jnp.arange(size)[None, :]).astype(jnp.float32)
        rows = jnp.einsum("bs,s...->b...", order, stacked, precision=HIGH)
        rows = rows.reshape((-1,) + rows.shape[2:])
        stride *= size
    return rows


def shards(
    slab_inverse, coupling, injection, neighbors, mode_shift, mode_table, emit_weight, absorb_weight
):
    pairs = slab_pairs(slab_inverse[0], coupling[0], injection[0], neighbors)
    local = pairs.shape[0]
    moms, groups = lax.axis_size("mom"), lax.axis_size("en")
    devices = moms * groups
    flat = pairs.reshape(local, -1)
    width = flat.shape[1] // devices
    blocks = jnp.swapaxes(flat.reshape(local, devices, width), 0, 1)
    table = gather_rows(mode_table[0].astype(jnp.float32)[None], "mom").astype(jnp.int32)
    sent = lax.all_to_all(blocks, ("mom", "en"), 0, 0)
    data = sent.reshape(moms, groups * local, width)
    data = jnp.pad(data, ((0, 0), (SHIFT_MAX, SHIFT_MAX), (0, 0)))
    weights = shift_weights(table, mode_shift, emit_weight, absorb_weight)
    mixed = mix(data, weights, groups * local)
    mixed = mixed.reshape(devices, local, width)
    back = lax.all_to_all(mixed, ("mom", "en"), 0, 0)
    result = jnp.swapaxes(back, 0, 1).reshape(pairs.shape)
    return result[None]


def solution(mesh):
    placed = (
        P("mom", "en", None, None, None, None),
        P("mom", None, None, None, None),
        P("mom", "en", None, None),
        P(),
        P(),
        P("mom", None),
        P(),
        P(),
    )
    return jax.shard_map(
        shards,
        mesh=mesh,
        in_specs=placed,
        out_specs=P("mom", "en", None, None, None),
        check_vma=False,
    )
```

```python
import jax
import jax.numpy as jnp
from jax import lax
from jax.sharding import PartitionSpec as P

SHIFT_MAX = 2
OFFSETS = (-2, -1, 1, 2)


HIGH = lax.Precision.HIGHEST
CHAIN = lax.Precision.HIGH


def with_halo(x, sides, width):
    for axis, dim in sides:
        count, length = (lax.axis_size(axis), x.shape[dim])
        up = [(i, (i + 1) % count) for i in range(count - 1)]
        down = [(j, i) for i, j in up]
        last = lax.slice_in_dim(x, length - width, length, axis=dim)
        leading = lax.slice_in_dim(x, 0, width, axis=dim)
        before = lax.ppermute(last, axis, up)
        after = lax.ppermute(leading, axis, down)
        x = jnp.concatenate([before, x, after], axis=dim)
    return x


def block(value):
    real, imag = value[..., 0, :, :], value[..., 1, :, :]
    top = jnp.concatenate([real, -imag], axis=-1)
    bottom = jnp.concatenate([imag, real], axis=-1)
    return jnp.concatenate([top, bottom], axis=-2)


def column(value, adjoint=False):
    real, imag = value[..., 0, :, :], value[..., 1, :, :]
    if adjoint:
        return jnp.concatenate([real, -imag], axis=-1)
    return jnp.concatenate([real, imag], axis=-2)


def split(value):
    rows = value.shape[-2] // 2
    return value.reshape(value.shape[:-2] + (2, rows, value.shape[-1]))


def cmul(left, right, spec="...ij,...jk->...ik", adjoint=False):
    if adjoint:
        spec = spec.replace("jk->", "kj->")
    product = jnp.einsum(spec, block(left), column(right, adjoint), precision=CHAIN)
    return split(product)


def slab_pairs(slab_inverse, coupling, injection, neighbors):
    orbitals = slab_inverse.shape[-1]
    slab_count = slab_inverse.shape[1]
    eye = jnp.eye(orbitals, dtype=jnp.float32)
    retarded = slab_inverse[:, 0]
    source = injection[:, 0][:, None, None, :]
    lesser = cmul(retarded * source, retarded, adjoint=True)
    collected = [lesser]
    for slab in range(1, slab_count):
        inverse = slab_inverse[:, slab]
        link = coupling[slab]
        both = jnp.concatenate([retarded, lesser], axis=-1)
        linked = cmul(link, both, "ij,ejk->eik")
        linked = jnp.stack([linked[..., :orbitals], linked[..., orbitals:]], axis=1)
        sandwich = cmul(linked, link, "ewij,jk->ewik", adjoint=True)
        sigma, middle = sandwich[:, 0], sandwich[:, 1]
        diagonal = eye[None] * injection[:, slab][:, None, :]
        middle = jnp.stack([middle[:, 0] + diagonal, middle[:, 1]], axis=1)
        inner = cmul(cmul(inverse, sigma), inverse)
        retarded = inverse + inner
        lesser = cmul(cmul(retarded, middle), retarded, adjoint=True)
        collected.append(lesser)
    stacked = jnp.stack(collected, axis=1)
    pieces = []
    rest = stacked
    for _ in range(3):
        piece = lax.reduce_precision(rest, exponent_bits=8, mantissa_bits=7)
        pieces.append(piece.astype(jnp.bfloat16))
        rest = rest - piece
    columns = jnp.arange(orbitals, dtype=jnp.int32)
    selector = (neighbors[..., None] == columns).astype(jnp.bfloat16)
    picked = jnp.einsum(
        "qesxoc,sojc->qesjxo", jnp.stack(pieces), selector, preferred_element_type=jnp.float32
    )
    picked = picked[0] + picked[1] + picked[2]
    return picked.reshape(picked.shape[0], -1, picked.shape[3], picked.shape[4])


def shift_weights(table, mode_shift, emit_weight, absorb_weight):
    mode_ids = jnp.arange(mode_shift.shape[0], dtype=jnp.int32)
    chosen = (table[..., None] == mode_ids).astype(jnp.float32)
    shift = jnp.sum(chosen * mode_shift.astype(jnp.float32), axis=-1)
    emit = jnp.sum(chosen * emit_weight, axis=-1)
    absorb = jnp.sum(chosen * absorb_weight, axis=-1)
    rows = []
    for offset in OFFSETS:
        if offset < 0:
            rows.append(emit * (shift == -offset).astype(jnp.float32))
        else:
            rows.append(absorb * (shift == offset).astype(jnp.float32))
    return jnp.stack(rows, axis=-2) / table.shape[-1]


def mix(data, weights, energies):
    windows = jnp.stack(
        [data[:, SHIFT_MAX + offset : SHIFT_MAX + offset + energies] for offset in OFFSETS]
    )
    return jnp.einsum("kdj,djec->kec", weights, windows, precision=HIGH)


def shards(
    slab_inverse, coupling, injection, neighbors, mode_shift, mode_table, emit_weight, absorb_weight
):
    pairs = slab_pairs(slab_inverse[0], coupling[0], injection[0], neighbors)
    local = pairs.shape[0]
    moms, groups = lax.axis_size("mom"), lax.axis_size("en")
    devices = moms * groups
    flat = pairs.reshape(local, -1)
    width = flat.shape[1] // devices
    blocks = jnp.swapaxes(flat.reshape(local, devices, width), 0, 1).reshape(devices, -1)
    share = -(-moms // groups)
    ids = jnp.pad(mode_table[0].astype(jnp.float32), (0, share * groups - moms))
    mine = lax.dynamic_slice_in_dim(ids, lax.axis_index("en") * share, share)
    rows = jnp.broadcast_to(mine[None], (devices, share))
    sent = lax.all_to_all(jnp.concatenate([blocks, rows], axis=1), ("mom", "en"), 0, 0)
    sent = sent.reshape(moms, groups, -1)
    data = sent[:, :, : local * width].reshape(moms, groups * local, width)
    data = jnp.pad(data, ((0, 0), (SHIFT_MAX, SHIFT_MAX), (0, 0)))
    table = sent[:, :, local * width :].reshape(moms, -1)[:, :moms].astype(jnp.int32)
    weights = shift_weights(table, mode_shift, emit_weight, absorb_weight)
    mixed = mix(data, weights, groups * local)
    mixed = mixed.reshape(devices, local, width)
    back = lax.all_to_all(mixed, ("mom", "en"), 0, 0)
    result = jnp.swapaxes(back, 0, 1).reshape(pairs.shape)
    return result[None]


def solution(mesh):
    placed = (
        P("mom", "en", None, None, None, None),
        P("mom", None, None, None, None),
        P("mom", "en", None, None),
        P(),
        P(),
        P("mom", None),
        P(),
        P(),
    )
    return jax.shard_map(
        shards,
        mesh=mesh,
        in_specs=placed,
        out_specs=P("mom", "en", None, None, None),
        check_vma=False,
    )
```

```python
import jax
import jax.numpy as jnp
from jax import lax
from jax.sharding import PartitionSpec as P

SHIFT_MAX = 2
OFFSETS = (-2, -1, 1, 2)


HIGH = lax.Precision.HIGHEST
CHAIN = lax.Precision.HIGH
PIECES = 2


def with_halo(x, sides, width):
    for axis, dim in sides:
        count, length = (lax.axis_size(axis), x.shape[dim])
        up = [(i, (i + 1) % count) for i in range(count - 1)]
        down = [(j, i) for i, j in up]
        last = lax.slice_in_dim(x, length - width, length, axis=dim)
        leading = lax.slice_in_dim(x, 0, width, axis=dim)
        before = lax.ppermute(last, axis, up)
        after = lax.ppermute(leading, axis, down)
        x = jnp.concatenate([before, x, after], axis=dim)
    return x


def block(value):
    real, imag = value[..., 0, :, :], value[..., 1, :, :]
    top = jnp.concatenate([real, -imag], axis=-1)
    bottom = jnp.concatenate([imag, real], axis=-1)
    return jnp.concatenate([top, bottom], axis=-2)


def column(value, adjoint=False):
    real, imag = value[..., 0, :, :], value[..., 1, :, :]
    if adjoint:
        return jnp.concatenate([real, -imag], axis=-1)
    return jnp.concatenate([real, imag], axis=-2)


def split(value):
    rows = value.shape[-2] // 2
    return value.reshape(value.shape[:-2] + (2, rows, value.shape[-1]))


def cmul(left, right, spec="...ij,...jk->...ik", adjoint=False):
    if adjoint:
        spec = spec.replace("jk->", "kj->")
    product = jnp.einsum(spec, block(left), column(right, adjoint), precision=CHAIN)
    return split(product)


def slab_pairs(slab_inverse, coupling, injection, neighbors):
    orbitals = slab_inverse.shape[-1]
    slab_count = slab_inverse.shape[1]
    eye = jnp.eye(orbitals, dtype=jnp.float32)
    retarded = slab_inverse[:, 0]
    source = injection[:, 0][:, None, None, :]
    lesser = cmul(retarded * source, retarded, adjoint=True)
    collected = [lesser]
    for slab in range(1, slab_count):
        inverse = slab_inverse[:, slab]
        link = coupling[slab]
        both = jnp.concatenate([retarded, lesser], axis=-1)
        linked = cmul(link, both, "ij,ejk->eik")
        linked = jnp.stack([linked[..., :orbitals], linked[..., orbitals:]], axis=1)
        sandwich = cmul(linked, link, "ewij,jk->ewik", adjoint=True)
        sigma, middle = sandwich[:, 0], sandwich[:, 1]
        diagonal = eye[None] * injection[:, slab][:, None, :]
        middle = jnp.stack([middle[:, 0] + diagonal, middle[:, 1]], axis=1)
        inner = cmul(cmul(inverse, sigma), inverse)
        retarded = inverse + inner
        lesser = cmul(cmul(retarded, middle), retarded, adjoint=True)
        collected.append(lesser)
    stacked = jnp.stack(collected, axis=1)
    pieces = []
    rest = stacked
    for _ in range(PIECES):
        piece = lax.reduce_precision(rest, exponent_bits=8, mantissa_bits=7)
        pieces.append(piece.astype(jnp.bfloat16))
        rest = rest - piece
    columns = jnp.arange(orbitals, dtype=jnp.int32)
    selector = (neighbors[..., None] == columns).astype(jnp.bfloat16)
    picked = jnp.einsum(
        "qesxoc,sojc->qesjxo", jnp.stack(pieces), selector, preferred_element_type=jnp.float32
    )
    picked = jnp.sum(picked, axis=0)
    return picked.reshape(picked.shape[0], -1, picked.shape[3], picked.shape[4])


def shift_weights(table, mode_shift, emit_weight, absorb_weight):
    mode_ids = jnp.arange(mode_shift.shape[0], dtype=jnp.int32)
    chosen = (table[..., None] == mode_ids).astype(jnp.float32)
    shift = jnp.sum(chosen * mode_shift.astype(jnp.float32), axis=-1)
    emit = jnp.sum(chosen * emit_weight, axis=-1)
    absorb = jnp.sum(chosen * absorb_weight, axis=-1)
    rows = []
    for offset in OFFSETS:
        if offset < 0:
            rows.append(emit * (shift == -offset).astype(jnp.float32))
        else:
            rows.append(absorb * (shift == offset).astype(jnp.float32))
    return jnp.stack(rows, axis=-2) / table.shape[-1]


def mix(data, weights, energies):
    windows = jnp.stack(
        [data[:, SHIFT_MAX + offset : SHIFT_MAX + offset + energies] for offset in OFFSETS]
    )
    return jnp.einsum("kdj,djec->kec", weights, windows, precision=HIGH)


def shards(
    slab_inverse, coupling, injection, neighbors, mode_shift, mode_table, emit_weight, absorb_weight
):
    pairs = slab_pairs(slab_inverse[0], coupling[0], injection[0], neighbors)
    local = pairs.shape[0]
    moms, groups = lax.axis_size("mom"), lax.axis_size("en")
    devices = moms * groups
    flat = pairs.reshape(local, -1)
    width = flat.shape[1] // devices
    blocks = jnp.swapaxes(flat.reshape(local, devices, width), 0, 1).reshape(devices, -1)
    share = -(-moms // groups)
    ids = jnp.pad(mode_table[0].astype(jnp.float32), (0, share * groups - moms))
    mine = lax.dynamic_slice_in_dim(ids, lax.axis_index("en") * share, share)
    rows = jnp.broadcast_to(mine[None], (devices, share))
    sent = lax.all_to_all(jnp.concatenate([blocks, rows], axis=1), ("mom", "en"), 0, 0)
    sent = sent.reshape(moms, groups, -1)
    data = sent[:, :, : local * width].reshape(moms, groups * local, width)
    data = jnp.pad(data, ((0, 0), (SHIFT_MAX, SHIFT_MAX), (0, 0)))
    table = sent[:, :, local * width :].reshape(moms, -1)[:, :moms].astype(jnp.int32)
    weights = shift_weights(table, mode_shift, emit_weight, absorb_weight)
    mixed = mix(data, weights, groups * local)
    mixed = mixed.reshape(devices, local, width)
    back = lax.all_to_all(mixed, ("mom", "en"), 0, 0)
    result = jnp.swapaxes(back, 0, 1).reshape(pairs.shape)
    return result[None]


def solution(mesh):
    placed = (
        P("mom", "en", None, None, None, None),
        P("mom", None, None, None, None),
        P("mom", "en", None, None),
        P(),
        P(),
        P("mom", None),
        P(),
        P(),
    )
    return jax.shard_map(
        shards,
        mesh=mesh,
        in_specs=placed,
        out_specs=P("mom", "en", None, None, None),
        check_vma=False,
    )
```

```python
import jax
import jax.numpy as jnp
from jax import lax
from jax.sharding import PartitionSpec as P

SHIFT_MAX = 2
OFFSETS = (-2, -1, 1, 2)


HIGH = lax.Precision.HIGHEST
CHAIN = lax.Precision.HIGH


def with_halo(x, sides, width):
    for axis, dim in sides:
        count, length = (lax.axis_size(axis), x.shape[dim])
        up = [(i, (i + 1) % count) for i in range(count - 1)]
        down = [(j, i) for i, j in up]
        last = lax.slice_in_dim(x, length - width, length, axis=dim)
        leading = lax.slice_in_dim(x, 0, width, axis=dim)
        before = lax.ppermute(last, axis, up)
        after = lax.ppermute(leading, axis, down)
        x = jnp.concatenate([before, x, after], axis=dim)
    return x


def block(value):
    real, imag = value[..., 0, :, :], value[..., 1, :, :]
    top = jnp.concatenate([real, -imag], axis=-1)
    bottom = jnp.concatenate([imag, real], axis=-1)
    return jnp.concatenate([top, bottom], axis=-2)


def column(value, adjoint=False):
    real, imag = value[..., 0, :, :], value[..., 1, :, :]
    if adjoint:
        return jnp.concatenate([real, -imag], axis=-1)
    return jnp.concatenate([real, imag], axis=-2)


def split(value):
    rows = value.shape[-2] // 2
    return value.reshape(value.shape[:-2] + (2, rows, value.shape[-1]))


def cmul(left, right, spec="...ij,...jk->...ik", adjoint=False):
    if adjoint:
        spec = spec.replace("jk->", "kj->")
    product = jnp.einsum(spec, block(left), column(right, adjoint), precision=CHAIN)
    return split(product)


def slab_pairs(slab_inverse, coupling, injection, neighbors):
    orbitals = slab_inverse.shape[-1]
    slab_count = slab_inverse.shape[1]
    eye = jnp.eye(orbitals, dtype=jnp.float32)
    retarded = slab_inverse[:, 0]
    source = injection[:, 0][:, None, None, :]
    lesser = cmul(retarded * source, retarded, adjoint=True)
    collected = [lesser]
    for slab in range(1, slab_count):
        inverse = slab_inverse[:, slab]
        link = coupling[slab]
        both = jnp.concatenate([retarded, lesser], axis=-1)
        linked = cmul(link, both, "ij,ejk->eik")
        linked = jnp.stack([linked[..., :orbitals], linked[..., orbitals:]], axis=1)
        sandwich = cmul(linked, link, "ewij,jk->ewik", adjoint=True)
        sigma, middle = sandwich[:, 0], sandwich[:, 1]
        diagonal = eye[None] * injection[:, slab][:, None, :]
        middle = jnp.stack([middle[:, 0] + diagonal, middle[:, 1]], axis=1)
        inner = cmul(cmul(inverse, sigma), inverse)
        retarded = inverse + inner
        lesser = cmul(cmul(retarded, middle), retarded, adjoint=True)
        collected.append(lesser)
    stacked = jnp.swapaxes(jnp.stack(collected, axis=1), -1, -2)
    columns = jnp.arange(orbitals, dtype=jnp.int32)
    chosen = jnp.swapaxes(neighbors, 1, 2)[:, :, None, :] == columns[:, None]
    picked = jnp.where(chosen[None, :, :, None], stacked[:, :, None], 0.0)
    picked = jnp.sum(picked, axis=4)
    return picked.reshape(picked.shape[0], -1, picked.shape[3], picked.shape[4])


def shift_weights(table, mode_shift, emit_weight, absorb_weight):
    mode_ids = jnp.arange(mode_shift.shape[0], dtype=jnp.int32)
    chosen = (table[..., None] == mode_ids).astype(jnp.float32)
    shift = jnp.sum(chosen * mode_shift.astype(jnp.float32), axis=-1)
    emit = jnp.sum(chosen * emit_weight, axis=-1)
    absorb = jnp.sum(chosen * absorb_weight, axis=-1)
    rows = []
    for offset in OFFSETS:
        if offset < 0:
            rows.append(emit * (shift == -offset).astype(jnp.float32))
        else:
            rows.append(absorb * (shift == offset).astype(jnp.float32))
    return jnp.stack(rows, axis=-2) / table.shape[-1]


def mix(data, weights, energies):
    windows = jnp.stack(
        [data[:, SHIFT_MAX + offset : SHIFT_MAX + offset + energies] for offset in OFFSETS]
    )
    return jnp.einsum("kdj,djec->kec", weights, windows, precision=HIGH)


def shards(
    slab_inverse, coupling, injection, neighbors, mode_shift, mode_table, emit_weight, absorb_weight
):
    pairs = slab_pairs(slab_inverse[0], coupling[0], injection[0], neighbors)
    local = pairs.shape[0]
    moms, groups = lax.axis_size("mom"), lax.axis_size("en")
    devices = moms * groups
    flat = pairs.reshape(local, -1)
    width = flat.shape[1] // devices
    blocks = jnp.swapaxes(flat.reshape(local, devices, width), 0, 1).reshape(devices, -1)
    share = -(-moms // groups)
    ids = jnp.pad(mode_table[0].astype(jnp.float32), (0, share * groups - moms))
    mine = lax.dynamic_slice_in_dim(ids, lax.axis_index("en") * share, share)
    rows = jnp.broadcast_to(mine[None], (devices, share))
    sent = lax.all_to_all(jnp.concatenate([blocks, rows], axis=1), ("mom", "en"), 0, 0)
    sent = sent.reshape(moms, groups, -1)
    data = sent[:, :, : local * width].reshape(moms, groups * local, width)
    data = jnp.pad(data, ((0, 0), (SHIFT_MAX, SHIFT_MAX), (0, 0)))
    table = sent[:, :, local * width :].reshape(moms, -1)[:, :moms].astype(jnp.int32)
    weights = shift_weights(table, mode_shift, emit_weight, absorb_weight)
    mixed = mix(data, weights, groups * local)
    mixed = mixed.reshape(devices, local, width)
    back = lax.all_to_all(mixed, ("mom", "en"), 0, 0)
    result = jnp.swapaxes(back, 0, 1).reshape(pairs.shape)
    return result[None]


def solution(mesh):
    placed = (
        P("mom", "en", None, None, None, None),
        P("mom", None, None, None, None),
        P("mom", "en", None, None),
        P(),
        P(),
        P("mom", None),
        P(),
        P(),
    )
    return jax.shard_map(
        shards,
        mesh=mesh,
        in_specs=placed,
        out_specs=P("mom", "en", None, None, None),
        check_vma=False,
    )
```

```python
import jax
import jax.numpy as jnp
from jax import lax
from jax.sharding import PartitionSpec as P

SHIFT_MAX = 2
OFFSETS = (-2, -1, 1, 2)


HIGH = lax.Precision.HIGHEST
CHAIN = lax.Precision.HIGH


def with_halo(x, sides, width):
    for axis, dim in sides:
        count, length = (lax.axis_size(axis), x.shape[dim])
        up = [(i, (i + 1) % count) for i in range(count - 1)]
        down = [(j, i) for i, j in up]
        last = lax.slice_in_dim(x, length - width, length, axis=dim)
        leading = lax.slice_in_dim(x, 0, width, axis=dim)
        before = lax.ppermute(last, axis, up)
        after = lax.ppermute(leading, axis, down)
        x = jnp.concatenate([before, x, after], axis=dim)
    return x


def block(value):
    real, imag = value[..., 0, :, :], value[..., 1, :, :]
    top = jnp.concatenate([real, -imag], axis=-1)
    bottom = jnp.concatenate([imag, real], axis=-1)
    return jnp.concatenate([top, bottom], axis=-2)


def column(value, adjoint=False):
    real, imag = value[..., 0, :, :], value[..., 1, :, :]
    if adjoint:
        return jnp.concatenate([real, -imag], axis=-1)
    return jnp.concatenate([real, imag], axis=-2)


def split(value):
    rows = value.shape[-2] // 2
    return value.reshape(value.shape[:-2] + (2, rows, value.shape[-1]))


def cmul(left, right, spec="...ij,...jk->...ik", adjoint=False):
    if adjoint:
        spec = spec.replace("jk->", "kj->")
    product = jnp.einsum(spec, block(left), column(right, adjoint), precision=CHAIN)
    return split(product)


def slab_pairs(slab_inverse, coupling, injection, neighbors):
    orbitals = slab_inverse.shape[-1]
    slab_count = slab_inverse.shape[1]
    eye = jnp.eye(orbitals, dtype=jnp.float32)
    retarded = slab_inverse[:, 0]
    source = injection[:, 0][:, None, None, :]
    lesser = cmul(retarded * source, retarded, adjoint=True)
    collected = [lesser]
    for slab in range(1, slab_count):
        inverse = slab_inverse[:, slab]
        link = coupling[slab]
        both = jnp.concatenate([retarded, lesser], axis=-1)
        linked = cmul(link, both, "ij,ejk->eik")
        linked = jnp.stack([linked[..., :orbitals], linked[..., orbitals:]], axis=1)
        sandwich = cmul(linked, link, "ewij,jk->ewik", adjoint=True)
        sigma, middle = sandwich[:, 0], sandwich[:, 1]
        diagonal = eye[None] * injection[:, slab][:, None, :]
        middle = jnp.stack([middle[:, 0] + diagonal, middle[:, 1]], axis=1)
        inner = cmul(cmul(inverse, sigma), inverse)
        retarded = inverse + inner
        lesser = cmul(cmul(retarded, middle), retarded, adjoint=True)
        collected.append(lesser)
    stacked = jnp.stack(collected, axis=1)
    pieces = []
    rest = stacked
    for _ in range(3):
        piece = lax.reduce_precision(rest, exponent_bits=8, mantissa_bits=7)
        pieces.append(piece.astype(jnp.bfloat16))
        rest = rest - piece
    columns = jnp.arange(orbitals, dtype=jnp.int32)
    selector = (neighbors[..., None] == columns).astype(jnp.bfloat16)
    picked = jnp.einsum(
        "qesxoc,sojc->qesjxo", jnp.stack(pieces), selector, preferred_element_type=jnp.float32
    )
    picked = picked[0] + picked[1] + picked[2]
    return picked.reshape(picked.shape[0], -1, picked.shape[3], picked.shape[4])


def shift_weights(table, mode_shift, emit_weight, absorb_weight):
    mode_ids = jnp.arange(mode_shift.shape[0], dtype=jnp.int32)
    chosen = (table[..., None] == mode_ids).astype(jnp.float32)
    shift = jnp.sum(chosen * mode_shift.astype(jnp.float32), axis=-1)
    emit = jnp.sum(chosen * emit_weight, axis=-1)
    absorb = jnp.sum(chosen * absorb_weight, axis=-1)
    rows = []
    for offset in OFFSETS:
        if offset < 0:
            rows.append(emit * (shift == -offset).astype(jnp.float32))
        else:
            rows.append(absorb * (shift == offset).astype(jnp.float32))
    return jnp.stack(rows, axis=-2) / table.shape[-1]


def mix(data, weights, energies):
    windows = jnp.stack(
        [data[:, SHIFT_MAX + offset : SHIFT_MAX + offset + energies] for offset in OFFSETS]
    )
    return jnp.einsum("kdj,djec->kec", weights, windows, precision=HIGH)


def shards(
    slab_inverse, coupling, injection, neighbors, mode_shift, mode_table, emit_weight, absorb_weight
):
    pairs = slab_pairs(slab_inverse[0], coupling[0], injection[0], neighbors)
    local = pairs.shape[0]
    moms, groups = lax.axis_size("mom"), lax.axis_size("en")
    flat = pairs.reshape(local, -1)
    width = flat.shape[1] // moms
    blocks = jnp.swapaxes(flat.reshape(local, moms, width), 0, 1).reshape(moms, -1)
    ids = jnp.broadcast_to(mode_table[0].astype(jnp.float32)[None], (moms, moms))
    sent = lax.all_to_all(jnp.concatenate([blocks, ids], axis=1), "mom", 0, 0)
    data = sent[:, : local * width].reshape(moms, local, width)
    table = sent[:, local * width :].astype(jnp.int32)
    weights = shift_weights(table, mode_shift, emit_weight, absorb_weight)
    reach = local + 2 * SHIFT_MAX
    data = jnp.pad(data, ((0, 0), (2 * SHIFT_MAX, 2 * SHIFT_MAX), (0, 0)))
    windows = jnp.stack(
        [data[:, SHIFT_MAX + offset : SHIFT_MAX + offset + reach] for offset in OFFSETS]
    )
    part = jnp.einsum("kdj,djec->kec", weights, windows, precision=HIGH)
    down = [(i, i - 1) for i in range(1, groups)]
    up = [(i, i + 1) for i in range(groups - 1)]
    from_up = lax.ppermute(part[:, :SHIFT_MAX], "en", down)
    from_down = lax.ppermute(part[:, SHIFT_MAX + local :], "en", up)
    own = part[:, SHIFT_MAX : SHIFT_MAX + local] + from_up + from_down
    back = lax.all_to_all(own, "mom", 0, 0)
    result = jnp.swapaxes(back, 0, 1).reshape(pairs.shape)
    return result[None]


def solution(mesh):
    placed = (
        P("mom", "en", None, None, None, None),
        P("mom", None, None, None, None),
        P("mom", "en", None, None),
        P(),
        P(),
        P("mom", None),
        P(),
        P(),
    )
    return jax.shard_map(
        shards,
        mesh=mesh,
        in_specs=placed,
        out_specs=P("mom", "en", None, None, None),
        check_vma=False,
    )
```

```python
import jax
import jax.numpy as jnp
from jax import lax
from jax.sharding import PartitionSpec as P

SHIFT_MAX = 2
OFFSETS = (-2, -1, 1, 2)


HIGH = lax.Precision.HIGHEST
CHAIN = lax.Precision.HIGH


def with_halo(x, sides, width):
    for axis, dim in sides:
        count, length = (lax.axis_size(axis), x.shape[dim])
        up = [(i, (i + 1) % count) for i in range(count - 1)]
        down = [(j, i) for i, j in up]
        last = lax.slice_in_dim(x, length - width, length, axis=dim)
        leading = lax.slice_in_dim(x, 0, width, axis=dim)
        before = lax.ppermute(last, axis, up)
        after = lax.ppermute(leading, axis, down)
        x = jnp.concatenate([before, x, after], axis=dim)
    return x


def block(value):
    real, imag = value[..., 0, :, :], value[..., 1, :, :]
    top = jnp.concatenate([real, -imag], axis=-1)
    bottom = jnp.concatenate([imag, real], axis=-1)
    return jnp.concatenate([top, bottom], axis=-2)


def column(value, adjoint=False):
    real, imag = value[..., 0, :, :], value[..., 1, :, :]
    if adjoint:
        return jnp.concatenate([real, -imag], axis=-1)
    return jnp.concatenate([real, imag], axis=-2)


def split(value):
    rows = value.shape[-2] // 2
    return value.reshape(value.shape[:-2] + (2, rows, value.shape[-1]))


def cmul(left, right, spec="...ij,...jk->...ik", adjoint=False):
    if adjoint:
        spec = spec.replace("jk->", "kj->")
    product = jnp.einsum(spec, block(left), column(right, adjoint), precision=CHAIN)
    return split(product)


def slab_pairs(slab_inverse, coupling, injection, neighbors):
    orbitals = slab_inverse.shape[-1]
    slab_count = slab_inverse.shape[1]
    eye = jnp.eye(orbitals, dtype=jnp.float32)
    retarded = slab_inverse[:, 0]
    source = injection[:, 0][:, None, None, :]
    lesser = cmul(retarded * source, retarded, adjoint=True)
    collected = [lesser]
    for slab in range(1, slab_count):
        inverse = slab_inverse[:, slab]
        link = coupling[slab]
        both = jnp.concatenate([retarded, lesser], axis=-1)
        linked = cmul(link, both, "ij,ejk->eik")
        linked = jnp.stack([linked[..., :orbitals], linked[..., orbitals:]], axis=1)
        sandwich = cmul(linked, link, "ewij,jk->ewik", adjoint=True)
        sigma, middle = sandwich[:, 0], sandwich[:, 1]
        diagonal = eye[None] * injection[:, slab][:, None, :]
        middle = jnp.stack([middle[:, 0] + diagonal, middle[:, 1]], axis=1)
        inner = cmul(cmul(inverse, sigma), inverse)
        retarded = inverse + inner
        lesser = cmul(cmul(retarded, middle), retarded, adjoint=True)
        collected.append(lesser)
    stacked = jnp.stack(collected, axis=1)
    pieces = []
    rest = stacked
    for _ in range(3):
        piece = lax.reduce_precision(rest, exponent_bits=8, mantissa_bits=7)
        pieces.append(piece.astype(jnp.bfloat16))
        rest = rest - piece
    columns = jnp.arange(orbitals, dtype=jnp.int32)
    selector = (neighbors[..., None] == columns).astype(jnp.bfloat16)
    picked = jnp.einsum(
        "qesxoc,sojc->qesjxo", jnp.stack(pieces), selector, preferred_element_type=jnp.float32
    )
    picked = picked[0] + picked[1] + picked[2]
    return picked.reshape(picked.shape[0], -1, picked.shape[3], picked.shape[4])


def shift_weights(table, mode_shift, emit_weight, absorb_weight):
    mode_ids = jnp.arange(mode_shift.shape[0], dtype=jnp.int32)
    chosen = (table[..., None] == mode_ids).astype(jnp.float32)
    shift = jnp.sum(chosen * mode_shift.astype(jnp.float32), axis=-1)
    emit = jnp.sum(chosen * emit_weight, axis=-1)
    absorb = jnp.sum(chosen * absorb_weight, axis=-1)
    rows = []
    for offset in OFFSETS:
        if offset < 0:
            rows.append(emit * (shift == -offset).astype(jnp.float32))
        else:
            rows.append(absorb * (shift == offset).astype(jnp.float32))
    return jnp.stack(rows, axis=-2) / table.shape[-1]


def mix(data, weights, energies):
    windows = jnp.stack(
        [data[:, SHIFT_MAX + offset : SHIFT_MAX + offset + energies] for offset in OFFSETS]
    )
    return jnp.einsum("kdj,djec->kec", weights, windows, precision=HIGH)


def shards(
    slab_inverse, coupling, injection, neighbors, mode_shift, mode_table, emit_weight, absorb_weight
):
    pairs = slab_pairs(slab_inverse[0], coupling[0], injection[0], neighbors)
    local = pairs.shape[0]
    moms, groups = lax.axis_size("mom"), lax.axis_size("en")
    flat = pairs.reshape(local, -1)
    width = flat.shape[1] // moms
    blocks = jnp.swapaxes(flat.reshape(local, moms, width), 0, 1).reshape(moms, -1)
    ids = jnp.broadcast_to(mode_table[0].astype(jnp.float32)[None], (moms, moms))
    sent = lax.all_to_all(jnp.concatenate([blocks, ids], axis=1), "mom", 0, 0)
    data = sent[:, : local * width].reshape(moms, local, width)
    table = sent[:, local * width :].astype(jnp.int32)
    weights = shift_weights(table, mode_shift, emit_weight, absorb_weight)
    reach = local + 2 * SHIFT_MAX
    data = jnp.pad(data, ((0, 0), (2 * SHIFT_MAX, 2 * SHIFT_MAX), (0, 0)))
    windows = jnp.stack(
        [data[:, SHIFT_MAX + offset : SHIFT_MAX + offset + reach] for offset in OFFSETS]
    )
    edges = jnp.concatenate([windows[:, :, :SHIFT_MAX], windows[:, :, SHIFT_MAX + local :]], axis=2)
    edge = jnp.einsum("kdj,djec->kec", weights, edges, precision=HIGH)
    down = [(i, i - 1) for i in range(1, groups)]
    up = [(i, i + 1) for i in range(groups - 1)]
    from_up = lax.ppermute(edge[:, :SHIFT_MAX], "en", down)
    from_down = lax.ppermute(edge[:, SHIFT_MAX:], "en", up)
    inside = windows[:, :, SHIFT_MAX : SHIFT_MAX + local]
    own = lax.optimization_barrier(jnp.einsum("kdj,djec->kec", weights, inside, precision=HIGH))
    own = own + from_up + from_down
    back = lax.all_to_all(own, "mom", 0, 0)
    result = jnp.swapaxes(back, 0, 1).reshape(pairs.shape)
    return result[None]


def solution(mesh):
    placed = (
        P("mom", "en", None, None, None, None),
        P("mom", None, None, None, None),
        P("mom", "en", None, None),
        P(),
        P(),
        P("mom", None),
        P(),
        P(),
    )
    return jax.shard_map(
        shards,
        mesh=mesh,
        in_specs=placed,
        out_specs=P("mom", "en", None, None, None),
        check_vma=False,
    )
```

```python
import jax
import jax.numpy as jnp
from jax import lax
from jax.sharding import PartitionSpec as P

SHIFT_MAX = 2
OFFSETS = (-2, -1, 1, 2)


HIGH = lax.Precision.HIGHEST
CHAIN = lax.Precision.HIGH


def with_halo(x, sides, width):
    for axis, dim in sides:
        count, length = (lax.axis_size(axis), x.shape[dim])
        up = [(i, (i + 1) % count) for i in range(count - 1)]
        down = [(j, i) for i, j in up]
        last = lax.slice_in_dim(x, length - width, length, axis=dim)
        leading = lax.slice_in_dim(x, 0, width, axis=dim)
        before = lax.ppermute(last, axis, up)
        after = lax.ppermute(leading, axis, down)
        x = jnp.concatenate([before, x, after], axis=dim)
    return x


def block(value):
    real, imag = value[..., 0, :, :], value[..., 1, :, :]
    top = jnp.concatenate([real, -imag], axis=-1)
    bottom = jnp.concatenate([imag, real], axis=-1)
    return jnp.concatenate([top, bottom], axis=-2)


def column(value, adjoint=False):
    real, imag = value[..., 0, :, :], value[..., 1, :, :]
    if adjoint:
        return jnp.concatenate([real, -imag], axis=-1)
    return jnp.concatenate([real, imag], axis=-2)


def split(value):
    rows = value.shape[-2] // 2
    return value.reshape(value.shape[:-2] + (2, rows, value.shape[-1]))


def cmul(left, right, spec="...ij,...jk->...ik", adjoint=False):
    if adjoint:
        spec = spec.replace("jk->", "kj->")
    product = jnp.einsum(spec, block(left), column(right, adjoint), precision=CHAIN)
    return split(product)


def slab_pairs(slab_inverse, coupling, injection, neighbors):
    orbitals = slab_inverse.shape[-1]
    slab_count = slab_inverse.shape[1]
    eye = jnp.eye(orbitals, dtype=jnp.float32)
    retarded = slab_inverse[:, 0]
    source = injection[:, 0][:, None, None, :]
    lesser = cmul(retarded * source, retarded, adjoint=True)
    collected = [lesser]
    for slab in range(1, slab_count):
        inverse = slab_inverse[:, slab]
        link = coupling[slab]
        both = jnp.concatenate([retarded, lesser], axis=-1)
        linked = cmul(link, both, "ij,ejk->eik")
        linked = jnp.stack([linked[..., :orbitals], linked[..., orbitals:]], axis=1)
        sandwich = cmul(linked, link, "ewij,jk->ewik", adjoint=True)
        sigma, middle = sandwich[:, 0], sandwich[:, 1]
        diagonal = eye[None] * injection[:, slab][:, None, :]
        middle = jnp.stack([middle[:, 0] + diagonal, middle[:, 1]], axis=1)
        inner = cmul(cmul(inverse, sigma), inverse)
        retarded = inverse + inner
        lesser = cmul(cmul(retarded, middle), retarded, adjoint=True)
        collected.append(lesser)
    stacked = jnp.stack(collected, axis=1)
    pieces = []
    rest = stacked
    for _ in range(3):
        piece = lax.reduce_precision(rest, exponent_bits=8, mantissa_bits=7)
        pieces.append(piece.astype(jnp.bfloat16))
        rest = rest - piece
    columns = jnp.arange(orbitals, dtype=jnp.int32)
    selector = (neighbors[..., None] == columns).astype(jnp.bfloat16)
    picked = jnp.einsum(
        "qesxoc,sojc->qesjxo", jnp.stack(pieces), selector, preferred_element_type=jnp.float32
    )
    picked = picked[0] + picked[1] + picked[2]
    return picked.reshape(picked.shape[0], -1, picked.shape[3], picked.shape[4])


def shift_weights(table, mode_shift, emit_weight, absorb_weight):
    mode_ids = jnp.arange(mode_shift.shape[0], dtype=jnp.int32)
    chosen = (table[..., None] == mode_ids).astype(jnp.float32)
    shift = jnp.sum(chosen * mode_shift.astype(jnp.float32), axis=-1)
    emit = jnp.sum(chosen * emit_weight, axis=-1)
    absorb = jnp.sum(chosen * absorb_weight, axis=-1)
    rows = []
    for offset in OFFSETS:
        if offset < 0:
            rows.append(emit * (shift == -offset).astype(jnp.float32))
        else:
            rows.append(absorb * (shift == offset).astype(jnp.float32))
    return jnp.stack(rows, axis=-2) / table.shape[-1]


def mix(data, weights, energies):
    windows = jnp.stack(
        [data[:, SHIFT_MAX + offset : SHIFT_MAX + offset + energies] for offset in OFFSETS]
    )
    return jnp.einsum("kdj,djec->kec", weights, windows, precision=HIGH)


def shards(
    slab_inverse, coupling, injection, neighbors, mode_shift, mode_table, emit_weight, absorb_weight
):
    pairs = slab_pairs(slab_inverse[0], coupling[0], injection[0], neighbors)
    local = pairs.shape[0]
    moms, groups = lax.axis_size("mom"), lax.axis_size("en")
    flat = pairs.reshape(local, -1)
    width = flat.shape[1] // moms
    blocks = jnp.swapaxes(flat.reshape(local, moms, width), 0, 1).reshape(moms, -1)
    ids = jnp.broadcast_to(mode_table[0].astype(jnp.float32)[None], (moms, moms))
    sent = lax.all_to_all(jnp.concatenate([blocks, ids], axis=1), "mom", 0, 0)
    data = sent[:, : local * width].reshape(moms, local, width)
    table = sent[:, local * width :].astype(jnp.int32)
    weights = shift_weights(table, mode_shift, emit_weight, absorb_weight)
    reach = local + 2 * SHIFT_MAX
    data = jnp.pad(data, ((0, 0), (2 * SHIFT_MAX, 2 * SHIFT_MAX), (0, 0)))
    windows = jnp.stack(
        [data[:, SHIFT_MAX + offset : SHIFT_MAX + offset + reach] for offset in OFFSETS]
    )
    part = jnp.einsum("kdj,djec->kec", weights, windows, precision=CHAIN)
    down = [(i, i - 1) for i in range(1, groups)]
    up = [(i, i + 1) for i in range(groups - 1)]
    from_up = lax.ppermute(part[:, :SHIFT_MAX], "en", down)
    from_down = lax.ppermute(part[:, SHIFT_MAX + local :], "en", up)
    own = part[:, SHIFT_MAX : SHIFT_MAX + local] + from_up + from_down
    back = lax.all_to_all(own, "mom", 0, 0)
    result = jnp.swapaxes(back, 0, 1).reshape(pairs.shape)
    return result[None]


def solution(mesh):
    placed = (
        P("mom", "en", None, None, None, None),
        P("mom", None, None, None, None),
        P("mom", "en", None, None),
        P(),
        P(),
        P("mom", None),
        P(),
        P(),
    )
    return jax.shard_map(
        shards,
        mesh=mesh,
        in_specs=placed,
        out_specs=P("mom", "en", None, None, None),
        check_vma=False,
    )
```

```python
import jax
import jax.numpy as jnp
from jax import lax
from jax.sharding import PartitionSpec as P

SHIFT_MAX = 2
OFFSETS = (-2, -1, 1, 2)


HIGH = lax.Precision.HIGHEST
CHAIN = lax.Precision.HIGH


def with_halo(x, sides, width):
    for axis, dim in sides:
        count, length = (lax.axis_size(axis), x.shape[dim])
        up = [(i, (i + 1) % count) for i in range(count - 1)]
        down = [(j, i) for i, j in up]
        last = lax.slice_in_dim(x, length - width, length, axis=dim)
        leading = lax.slice_in_dim(x, 0, width, axis=dim)
        before = lax.ppermute(last, axis, up)
        after = lax.ppermute(leading, axis, down)
        x = jnp.concatenate([before, x, after], axis=dim)
    return x


def block(value):
    real, imag = value[..., 0, :, :], value[..., 1, :, :]
    top = jnp.concatenate([real, -imag], axis=-1)
    bottom = jnp.concatenate([imag, real], axis=-1)
    return jnp.concatenate([top, bottom], axis=-2)


def column(value, adjoint=False):
    real, imag = value[..., 0, :, :], value[..., 1, :, :]
    if adjoint:
        return jnp.concatenate([real, -imag], axis=-1)
    return jnp.concatenate([real, imag], axis=-2)


def split(value):
    rows = value.shape[-2] // 2
    return value.reshape(value.shape[:-2] + (2, rows, value.shape[-1]))


def cmul(left, right, spec="...ij,...jk->...ik", adjoint=False):
    if adjoint:
        spec = spec.replace("jk->", "kj->")
    product = jnp.einsum(spec, block(left), column(right, adjoint), precision=CHAIN)
    return split(product)


def slab_pairs(slab_inverse, coupling, injection, neighbors):
    orbitals = slab_inverse.shape[-1]
    slab_count = slab_inverse.shape[1]
    eye = jnp.eye(orbitals, dtype=jnp.float32)
    retarded = slab_inverse[:, 0]
    source = injection[:, 0][:, None, None, :]
    lesser = cmul(retarded * source, retarded, adjoint=True)
    collected = [lesser]
    for slab in range(1, slab_count):
        inverse = slab_inverse[:, slab]
        link = coupling[slab]
        both = jnp.concatenate([retarded, lesser], axis=-1)
        linked = cmul(link, both, "ij,ejk->eik")
        linked = jnp.stack([linked[..., :orbitals], linked[..., orbitals:]], axis=1)
        sandwich = cmul(linked, link, "ewij,jk->ewik", adjoint=True)
        sigma, middle = sandwich[:, 0], sandwich[:, 1]
        diagonal = eye[None] * injection[:, slab][:, None, :]
        middle = jnp.stack([middle[:, 0] + diagonal, middle[:, 1]], axis=1)
        inner = cmul(cmul(inverse, sigma), inverse)
        retarded = inverse + inner
        lesser = cmul(cmul(retarded, middle), retarded, adjoint=True)
        collected.append(lesser)
    stacked = jnp.stack(collected, axis=1)
    pieces = []
    rest = stacked
    for _ in range(3):
        piece = lax.reduce_precision(rest, exponent_bits=8, mantissa_bits=7)
        pieces.append(piece.astype(jnp.bfloat16))
        rest = rest - piece
    columns = jnp.arange(orbitals, dtype=jnp.int32)
    selector = (neighbors[..., None] == columns).astype(jnp.bfloat16)
    picked = jnp.einsum(
        "qesxoc,sojc->qesjxo", jnp.stack(pieces), selector, preferred_element_type=jnp.float32
    )
    picked = picked[0] + picked[1] + picked[2]
    return picked.reshape(picked.shape[0], -1, picked.shape[3], picked.shape[4])


def shift_weights(table, mode_shift, emit_weight, absorb_weight):
    mode_ids = jnp.arange(mode_shift.shape[0], dtype=jnp.int32)
    chosen = (table[..., None] == mode_ids).astype(jnp.float32)
    shift = jnp.sum(chosen * mode_shift.astype(jnp.float32), axis=-1)
    emit = jnp.sum(chosen * emit_weight, axis=-1)
    absorb = jnp.sum(chosen * absorb_weight, axis=-1)
    rows = []
    for offset in OFFSETS:
        if offset < 0:
            rows.append(emit * (shift == -offset).astype(jnp.float32))
        else:
            rows.append(absorb * (shift == offset).astype(jnp.float32))
    return jnp.stack(rows, axis=-2) / table.shape[-1]


def mix(data, weights, energies):
    windows = jnp.stack(
        [data[:, SHIFT_MAX + offset : SHIFT_MAX + offset + energies] for offset in OFFSETS]
    )
    return jnp.einsum("kdj,djec->kec", weights, windows, precision=HIGH)


def shards(
    slab_inverse, coupling, injection, neighbors, mode_shift, mode_table, emit_weight, absorb_weight
):
    pairs = slab_pairs(slab_inverse[0], coupling[0], injection[0], neighbors)
    local = pairs.shape[0]
    moms, groups = lax.axis_size("mom"), lax.axis_size("en")
    flat = pairs.reshape(local, -1)
    width = flat.shape[1] // moms
    blocks = jnp.swapaxes(flat.reshape(local, moms, width), 0, 1).reshape(moms, -1)
    ids = jnp.broadcast_to(mode_table[0].astype(jnp.float32)[None], (moms, moms))
    sent = lax.all_to_all(jnp.concatenate([blocks, ids], axis=1), "mom", 0, 0)
    data = sent[:, : local * width].reshape(moms, local, width)
    table = sent[:, local * width :].astype(jnp.int32)
    weights = shift_weights(table, mode_shift, emit_weight, absorb_weight)
    reach = local + 2 * SHIFT_MAX
    data = jnp.pad(data, ((0, 0), (2 * SHIFT_MAX, 2 * SHIFT_MAX), (0, 0)))
    windows = jnp.stack(
        [data[:, SHIFT_MAX + offset : SHIFT_MAX + offset + reach] for offset in OFFSETS]
    )
    part = jnp.einsum("kdj,djec->kec", weights, windows, precision=CHAIN)
    down = [(i, (i - 1) % groups) for i in range(groups)]
    up = [(i, (i + 1) % groups) for i in range(groups)]
    place = lax.axis_index("en")
    from_up = lax.ppermute(part[:, :SHIFT_MAX], "en", down)
    from_up = jnp.where(place == groups - 1, 0.0, from_up)
    from_down = lax.ppermute(part[:, SHIFT_MAX + local :], "en", up)
    from_down = jnp.where(place == 0, 0.0, from_down)
    own = part[:, SHIFT_MAX : SHIFT_MAX + local] + from_up + from_down
    back = lax.all_to_all(own, "mom", 0, 0)
    result = jnp.swapaxes(back, 0, 1).reshape(pairs.shape)
    return result[None]


def solution(mesh):
    placed = (
        P("mom", "en", None, None, None, None),
        P("mom", None, None, None, None),
        P("mom", "en", None, None),
        P(),
        P(),
        P("mom", None),
        P(),
        P(),
    )
    return jax.shard_map(
        shards,
        mesh=mesh,
        in_specs=placed,
        out_specs=P("mom", "en", None, None, None),
        check_vma=False,
    )
```

```python
import jax
import jax.numpy as jnp
from jax import lax
from jax.sharding import PartitionSpec as P

SHIFT_MAX = 2
OFFSETS = (-2, -1, 1, 2)


HIGH = lax.Precision.HIGHEST
CHAIN = lax.Precision.HIGH


def with_halo(x, sides, width):
    for axis, dim in sides:
        count, length = (lax.axis_size(axis), x.shape[dim])
        up = [(i, (i + 1) % count) for i in range(count - 1)]
        down = [(j, i) for i, j in up]
        last = lax.slice_in_dim(x, length - width, length, axis=dim)
        leading = lax.slice_in_dim(x, 0, width, axis=dim)
        before = lax.ppermute(last, axis, up)
        after = lax.ppermute(leading, axis, down)
        x = jnp.concatenate([before, x, after], axis=dim)
    return x


def block(value):
    real, imag = value[..., 0, :, :], value[..., 1, :, :]
    top = jnp.concatenate([real, -imag], axis=-1)
    bottom = jnp.concatenate([imag, real], axis=-1)
    return jnp.concatenate([top, bottom], axis=-2)


def column(value, adjoint=False):
    real, imag = value[..., 0, :, :], value[..., 1, :, :]
    if adjoint:
        return jnp.concatenate([real, -imag], axis=-1)
    return jnp.concatenate([real, imag], axis=-2)


def split(value):
    rows = value.shape[-2] // 2
    return value.reshape(value.shape[:-2] + (2, rows, value.shape[-1]))


def cmul(left, right, spec="...ij,...jk->...ik", adjoint=False):
    if adjoint:
        spec = spec.replace("jk->", "kj->")
    product = jnp.einsum(spec, block(left), column(right, adjoint), precision=CHAIN)
    return split(product)


def slab_pairs(slab_inverse, coupling, injection, neighbors):
    orbitals = slab_inverse.shape[-1]
    slab_count = slab_inverse.shape[1]
    eye = jnp.eye(orbitals, dtype=jnp.float32)
    retarded = slab_inverse[:, 0]
    source = injection[:, 0][:, None, None, :]
    lesser = cmul(retarded * source, retarded, adjoint=True)
    collected = [lesser]
    for slab in range(1, slab_count):
        inverse = slab_inverse[:, slab]
        link = coupling[slab]
        both = jnp.concatenate([retarded, lesser], axis=-1)
        linked = cmul(link, both, "ij,ejk->eik")
        linked = jnp.stack([linked[..., :orbitals], linked[..., orbitals:]], axis=1)
        sandwich = cmul(linked, link, "ewij,jk->ewik", adjoint=True)
        sigma, middle = sandwich[:, 0], sandwich[:, 1]
        diagonal = eye[None] * injection[:, slab][:, None, :]
        middle = jnp.stack([middle[:, 0] + diagonal, middle[:, 1]], axis=1)
        inner = cmul(cmul(inverse, sigma), inverse)
        retarded = inverse + inner
        lesser = cmul(cmul(retarded, middle), retarded, adjoint=True)
        collected.append(lesser)
    stacked = jnp.stack(collected, axis=1)
    pieces = []
    rest = stacked
    for _ in range(3):
        piece = lax.reduce_precision(rest, exponent_bits=8, mantissa_bits=7)
        pieces.append(piece.astype(jnp.bfloat16))
        rest = rest - piece
    columns = jnp.arange(orbitals, dtype=jnp.int32)
    selector = (neighbors[..., None] == columns).astype(jnp.bfloat16)
    selector = jnp.concatenate([selector] * len(pieces), axis=-1)
    joined = jnp.concatenate(pieces, axis=-1)
    picked = jnp.einsum("esxok,sojk->esjxo", joined, selector, preferred_element_type=jnp.float32)
    return picked.reshape(picked.shape[0], -1, picked.shape[3], picked.shape[4])


def shift_weights(table, mode_shift, emit_weight, absorb_weight):
    mode_ids = jnp.arange(mode_shift.shape[0], dtype=jnp.int32)
    chosen = (table[..., None] == mode_ids).astype(jnp.float32)
    shift = jnp.sum(chosen * mode_shift.astype(jnp.float32), axis=-1)
    emit = jnp.sum(chosen * emit_weight, axis=-1)
    absorb = jnp.sum(chosen * absorb_weight, axis=-1)
    rows = []
    for offset in OFFSETS:
        if offset < 0:
            rows.append(emit * (shift == -offset).astype(jnp.float32))
        else:
            rows.append(absorb * (shift == offset).astype(jnp.float32))
    return jnp.stack(rows, axis=-2) / table.shape[-1]


def mix(data, weights, energies):
    windows = jnp.stack(
        [data[:, SHIFT_MAX + offset : SHIFT_MAX + offset + energies] for offset in OFFSETS]
    )
    return jnp.einsum("kdj,djec->kec", weights, windows, precision=HIGH)


def shards(
    slab_inverse, coupling, injection, neighbors, mode_shift, mode_table, emit_weight, absorb_weight
):
    pairs = slab_pairs(slab_inverse[0], coupling[0], injection[0], neighbors)
    local = pairs.shape[0]
    moms, groups = lax.axis_size("mom"), lax.axis_size("en")
    flat = pairs.reshape(local, -1)
    width = flat.shape[1] // moms
    blocks = jnp.swapaxes(flat.reshape(local, moms, width), 0, 1).reshape(moms, -1)
    ids = jnp.broadcast_to(mode_table[0].astype(jnp.float32)[None], (moms, moms))
    sent = lax.all_to_all(jnp.concatenate([blocks, ids], axis=1), "mom", 0, 0)
    data = sent[:, : local * width].reshape(moms, local, width)
    table = sent[:, local * width :].astype(jnp.int32)
    weights = shift_weights(table, mode_shift, emit_weight, absorb_weight)
    reach = local + 2 * SHIFT_MAX
    data = jnp.pad(data, ((0, 0), (2 * SHIFT_MAX, 2 * SHIFT_MAX), (0, 0)))
    windows = jnp.stack(
        [data[:, SHIFT_MAX + offset : SHIFT_MAX + offset + reach] for offset in OFFSETS]
    )
    part = jnp.einsum("kdj,djec->kec", weights, windows, precision=CHAIN)
    down = [(i, i - 1) for i in range(1, groups)]
    up = [(i, i + 1) for i in range(groups - 1)]
    from_up = lax.ppermute(part[:, :SHIFT_MAX], "en", down)
    from_down = lax.ppermute(part[:, SHIFT_MAX + local :], "en", up)
    own = part[:, SHIFT_MAX : SHIFT_MAX + local] + from_up + from_down
    back = lax.all_to_all(own, "mom", 0, 0)
    result = jnp.swapaxes(back, 0, 1).reshape(pairs.shape)
    return result[None]


def solution(mesh):
    placed = (
        P("mom", "en", None, None, None, None),
        P("mom", None, None, None, None),
        P("mom", "en", None, None),
        P(),
        P(),
        P("mom", None),
        P(),
        P(),
    )
    return jax.shard_map(
        shards,
        mesh=mesh,
        in_specs=placed,
        out_specs=P("mom", "en", None, None, None),
        check_vma=False,
    )
```
